32 devices in a mesh: grp: 2 (over x), section: 16 (over z, y, core).
Axes of the slice: x: 2, y: 2, z: 4, core: 2. Of those that a mesh axis runs over, the one named last changes fastest.
Arguments:
- latent: bfloat16 [1536, 64], P(('grp', 'section')), parts along dimension 0, may hold values from -6 to 6
- control_latent: bfloat16 [1536, 64], P(('grp', 'section')), parts along dimension 0, may hold values from -6 to 6
- patch_tiles: int32 [4], replicated, may hold values from 1 to 2, 6 in all
- tile_lists: int32 [2, 6, 3], replicated, may hold values from 0 to 5, as said below
- tile_counts: int32 [2, 6], replicated, may hold values from 1 to 3, as said below
- embed_weight: bfloat16 [64, 3072], replicated, may hold values from -0.75 to 0.75
- control_embed: bfloat16 [64, 3072], replicated, may hold values from -0.75 to 0.75
- modulation: float32 [2, 3, 3072], replicated, may hold values from -4 to 4
- qk_gain: float32 [2, 2, 128], replicated, may hold values from 0.1 to 1.9
- qkv_weight: bfloat16 [16, 3072, 1152], P('section'), may hold values from -0.109375 to 0.109375
- out_weight: bfloat16 [16, 384, 3072], P('section'), may hold values from -0.109375 to 0.109375
- stale_cache: bfloat16 [16, 1536, 768], P('section', 'grp'), parts along dimension 1, may hold values from -6 to 6
- control_gain: float32 [1, 3072], replicated, may hold values from -3 to 3
- final_mod: float32 [2, 3072], replicated, may hold values from -3 to 3
- final_weight: bfloat16 [3072, 64], replicated, may hold values from -0.109375 to 0.109375
Outputs:
- denoised: float32 [1536, 64], P(('grp', 'section')), parts along dimension 0
The draws below stay inside these ranges and needn't reach their ends.
There are 2 independent parts, one for each index of `grp`. The reference program is written for one: setup_inputs(seed, part) draws one part's arguments, and reference() takes and returns one part's arrays. A program takes and returns all parts, laid end to end along the dimension named above; an argument that names none is the same for every part. Nothing has to cross between parts.
Inputs may be any that keep to these rules, and one draw needn't show every extreme that they name: `patch_tiles`: the patches are contiguous and in order and together cover all 6 tiles; the largest has exactly 2 tiles. Entry 0 of tile_lists[b, t] is t itself; the 3 entries of one row are distinct. `tile_counts`: in every block slot some query tile uses all 3 listed tiles.
All inputs are finite; a program needn't handle non-finite values.
Results may differ from the reference program's by a relative error of at most 0.014.
Values may be sent and summed in bfloat16 or wider, within the bound.
No kernel may reach another device: no remote copies, remote signals or barrier semaphores. Data moves between devices by JAX's collectives and lax.ppermute only.
A program may use at most 64 MiB of HBM per device.

```python
import math
import jax
import jax.numpy as jnp
import numpy as np
from jax import lax

D = 3072
HEADS = 24
HD = 128
HG = 8
HEADS_DEV = 3
C_OUT = 64
TILE = 128
KSEL = 3
PATCHES = 4
TILES = 6
PMAX = 2
SEQ = 768
SLOTS = 2
CTRL = 1
MAIN = 1


def draw_tile_lists(key, part):
    random_part = jax.random.randint(jax.random.fold_in(key, 11), (SLOTS, TILES, TILES), 0, 2 ** 18)
    tile_ids = jnp.arange(TILES, dtype=jnp.int32)
    distance = jnp.abs(tile_ids[:, None] - tile_ids[None, :])
    ranking = (random_part + distance[None, :, :] * 2 ** 16) * TILES + tile_ids[None, None, :]
    ranking = jnp.where(distance[None, :, :] == 0, -1, ranking)
    ordering = jnp.argsort(ranking, axis=-1, stable=True)
    return ordering[:, :, :KSEL].astype(jnp.int32)


def draw_tile_counts(key, part):
    drawn = jax.random.randint(jax.random.fold_in(key, 21), (SLOTS, TILES), 1, KSEL + 1)
    forced = jax.random.randint(jax.random.fold_in(key, 22), (SLOTS, 1), 0, TILES)
    tile_ids = jnp.arange(TILES, dtype=jnp.int32)[None, :]
    return jnp.where(tile_ids == forced, KSEL, drawn).astype(jnp.int32)


def levels(key, shape, cuts, low, high):
    loudness = 1.0
    for dim, shards_of in cuts:
        draws = jax.random.uniform(jax.random.fold_in(jax.random.fold_in(key, 6), dim), (shards_of,), jnp.float32, low / len(cuts), high / len(cuts))
        loudness = loudness * jnp.repeat(jnp.exp(draws), shape[dim] // shards_of).reshape((-1,) + (1,) * (len(shape) - 1 - dim))
    return loudness


def profile(number_of, total, limit, slope):
    loads = [(1 << 20) // math.isqrt(rank ** slope) + 1 for rank in range(2, number_of + 1)]
    surplus, counts = total - limit - (number_of - 1), [1] * (number_of - 1)
    while surplus > 0:
        free = [i for i in range(number_of - 1) if counts[i] < limit]
        mass, remaining = sum([loads[i] for i in free]), surplus
        for i in free:
            more = min(limit - counts[i], max(1, remaining * loads[i] // mass), surplus)
            counts[i] = counts[i] + more
            surplus = surplus - more
    return np.array([limit] + counts)


def ragged_sizes(rng, count, total, reach, skew):
    if count == 2:
        one = jax.random.randint(rng, (), max(1, total - reach), min(reach, total - 1) + 1)
        return jnp.stack([one, total - one])
    tallies = jnp.asarray(profile(count, total, reach, skew), jnp.int32)
    pairs = (count - 1) // 2
    source_of, sink = tallies[1:1 + 2 * pairs:2], tallies[2:2 + 2 * pairs:2]
    room = jnp.minimum(source_of - 1, reach - sink)
    shifted = jax.random.randint(jax.random.fold_in(rng, 1), (pairs,), 0, 1 << 20) % (room + 1)
    tallies = tallies.at[1:1 + 2 * pairs:2].set(source_of - shifted).at[2:2 + 2 * pairs:2].set(sink + shifted)
    return tallies[jax.random.permutation(jax.random.fold_in(rng, 2), count)]


def centred(stream_key, shape, spread, bound, split=(), kind=jnp.bfloat16):
    values = jax.random.normal(stream_key, shape, jnp.float32) * spread
    if len(split) > 0:
        values = levels(stream_key, shape, split, -0.22, 0.18) * values
    return jnp.clip(values, min=-bound, max=bound).astype(kind)


def setup_inputs(seed: int = 0, part: int = 0) -> dict:
    key_list = jax.random.split(jax.random.key(seed), 16)
    part_splits = jax.random.split(jax.random.fold_in(key_list[15], part), 16)
    return {
        "latent": centred(part_splits[0], (SEQ, C_OUT), 1.0, 6.0, ((0, 16),)),
        "control_latent": centred(part_splits[1], (SEQ, C_OUT), 1.0, 6.0, ((0, 16),)),
        "patch_tiles": ragged_sizes(key_list[2], PATCHES, TILES, PMAX, 0).astype(jnp.int32),
        "tile_lists": draw_tile_lists(jax.random.fold_in(key_list[15], 71), part),
        "tile_counts": draw_tile_counts(jax.random.fold_in(key_list[15], 71), part),
        "embed_weight": centred(key_list[5], (C_OUT, D), C_OUT ** -0.5, 0.75),
        "control_embed": centred(key_list[6], (C_OUT, D), C_OUT ** -0.5, 0.75),
        "modulation": centred(key_list[7], (SLOTS, 3, D), 1.0, 4.0, (), jnp.float32),
        "qk_gain": jnp.clip(1.0 + 0.18 * jax.random.normal(key_list[8], (SLOTS, 2, HD), jnp.float32), 0.1, 1.9),
        "qkv_weight": centred(key_list[9], (SLOTS * HG, D, 3 * HEADS_DEV * HD), D ** -0.5, 0.109375, ((0, 16),)),
        "out_weight": centred(key_list[10], (SLOTS * HG, HEADS_DEV * HD, D), (HEADS * HD) ** -0.5, 0.109375, ((0, 16),)),
        "stale_cache": centred(part_splits[11], (SLOTS * HG, SEQ, 2 * HEADS_DEV * HD), 1.0, 6.0, ((0, 16),)),
        "control_gain": centred(key_list[12], (CTRL, D), 0.5, 3.0, (), jnp.float32),
        "final_mod": centred(key_list[13], (2, D), 0.5, 3.0, (), jnp.float32),
        "final_weight": centred(key_list[14], (D, C_OUT), D ** -0.5, 0.109375),
    }


EPSILON = 1e-06

def modulated(hidden, shift_row, scale_row):
    values = hidden.astype(jnp.float32)
    centered = values - lax.optimization_barrier(jnp.mean(values, axis=-1, keepdims=True))
    variance = lax.optimization_barrier(jnp.mean(centered * centered, axis=-1, keepdims=True))
    normed = centered * lax.rsqrt(variance + EPSILON)
    return (normed * (1.0 + scale_row) + shift_row).astype(jnp.bfloat16)

def rms_scaled(values, gain_row):
    return values * lax.rsqrt(lax.optimization_barrier(jnp.mean(values * values, axis=-1, keepdims=True)) + EPSILON) * gain_row

def attend_group(modded, w_qkv, w_out, memory, gain_pair, start_tile, patch_length, tile_list, tile_limit):
    row_count = modded.shape[0]
    query_tiles_count = row_count // TILE
    head_count = w_out.shape[0] // HD
    projected = jnp.dot(modded, w_qkv, preferred_element_type=jnp.float32).reshape(row_count, 3, head_count, HD)
    queries = rms_scaled(projected[:, 0], gain_pair[0]).astype(jnp.bfloat16)
    keys_new = rms_scaled(projected[:, 1], gain_pair[1]).astype(jnp.bfloat16)
    values_new = projected[:, 2].astype(jnp.bfloat16)
    fresh_rows = jnp.concatenate([keys_new.reshape(row_count, head_count * HD), values_new.reshape(row_count, head_count * HD)], axis=1)
    row_start = (start_tile * TILE).astype(jnp.int32)
    previous = lax.dynamic_slice_in_dim(memory, row_start, row_count, 0)
    live_rows = jnp.arange(row_count) < patch_length * TILE
    memory = lax.dynamic_update_slice_in_dim(memory, jnp.where(live_rows[:, None], fresh_rows, previous), row_start, 0)
    tiled_memory = memory.reshape(-1, TILE, 2, head_count, HD)
    query_tiles = jnp.minimum(start_tile + jnp.arange(query_tiles_count), TILES - 1).astype(jnp.int32)
    picked = tile_list[query_tiles]
    used_counts = tile_limit[query_tiles]
    chosen = tiled_memory[picked]
    key_rows = chosen[:, :, :, 0].reshape(query_tiles_count, KSEL * TILE, head_count, HD)
    value_rows = chosen[:, :, :, 1].reshape(query_tiles_count, KSEL * TILE, head_count, HD)
    query_rows = queries.reshape(query_tiles_count, TILE, head_count, HD)
    scores = jnp.einsum('tqhd,tkhd->thqk', query_rows.astype(jnp.float32), key_rows.astype(jnp.float32)) / math.sqrt(HD)
    allowed = (jnp.arange(KSEL * TILE) // TILE)[None, :] < used_counts[:, None]
    scores = jnp.where(allowed[:, None, None, :], scores, -1e+30)
    highest = lax.optimization_barrier(jnp.max(scores, axis=-1, keepdims=True))
    weights = jnp.exp(scores - highest)
    probabilities = (weights / lax.optimization_barrier(jnp.sum(weights, axis=-1, keepdims=True))).astype(jnp.bfloat16)
    attended = jnp.einsum('thqk,tkhd->tqhd', probabilities.astype(jnp.float32), value_rows.astype(jnp.float32)).astype(jnp.bfloat16)
    attended = attended.reshape(row_count, head_count * HD)
    partial_value = jnp.dot(attended, w_out, preferred_element_type=jnp.float32)
    return (partial_value, memory)

def reference(latent, control_latent, patch_tiles, tile_lists, tile_counts, embed_weight, control_embed, modulation, qk_gain, qkv_weight, out_weight, stale_cache, control_gain, final_mod, final_weight):
    row_count = PMAX * TILE
    padding = ((0, row_count), (0, 0))
    latent_pad = jnp.pad(latent, padding)
    control_pad = jnp.pad(control_latent, padding)
    memories = [jnp.pad(stale_cache[device_index], padding) for device_index in range(SLOTS * HG)]
    starts = jnp.cumsum(patch_tiles) - patch_tiles
    denoised = jnp.zeros((SEQ + row_count, C_OUT), jnp.float32)

    def apply_block(block_index, hidden, start_tile, patch_length):
        shifts = modulation[block_index]
        modded = modulated(hidden, shifts[0], shifts[1])
        summed = jnp.zeros((row_count, D), jnp.float32)
        for group_index in range(HG):
            device_index = block_index * HG + group_index
            partial_value, memories[device_index] = attend_group(modded, qkv_weight[device_index], out_weight[device_index], memories[device_index], qk_gain[block_index], start_tile, patch_length, tile_lists[block_index], tile_counts[block_index])
            rounded = lax.optimization_barrier(partial_value.astype(jnp.bfloat16))
            summed = summed + rounded.astype(jnp.float32)
        return hidden.astype(jnp.float32) + shifts[2] * summed
    for patch_index in range(PATCHES):
        start_tile = starts[patch_index]
        patch_length = patch_tiles[patch_index]
        row_start = (start_tile * TILE).astype(jnp.int32)
        own_latent = lax.dynamic_slice_in_dim(latent_pad, row_start, row_count, 0)
        own_control = lax.dynamic_slice_in_dim(control_pad, row_start, row_count, 0)
        embedded = jnp.dot(own_latent, embed_weight, preferred_element_type=jnp.float32)
        hidden = embedded.astype(jnp.bfloat16)
        control = (embedded + jnp.dot(own_control, control_embed, preferred_element_type=jnp.float32)).astype(jnp.bfloat16)
        for block_index in range(MAIN):
            control = apply_block(2 * block_index, control, start_tile, patch_length).astype(jnp.bfloat16)
            updated = apply_block(2 * block_index + 1, hidden, start_tile, patch_length)
            updated = updated + control_gain[block_index] * control.astype(jnp.float32)
            hidden = updated.astype(jnp.bfloat16)
        final_rows = jnp.dot(modulated(hidden, final_mod[0], final_mod[1]), final_weight, preferred_element_type=jnp.float32)
        previous = lax.dynamic_slice_in_dim(denoised, row_start, row_count, 0)
        live_rows = jnp.arange(row_count) < patch_length * TILE
        denoised = lax.dynamic_update_slice_in_dim(denoised, jnp.where(live_rows[:, None], final_rows, previous), row_start, 0)
    return denoised[:SEQ]
```

```python
import math

import jax
import jax.numpy as jnp
from jax import lax
from jax.sharding import PartitionSpec as P

HD = 128
HG = 8
TILE = 128

EPSILON = 1e-06


def from_partner(value, axis, distance):
    return lax.ppermute(value, axis, [(i, i ^ 1 << distance) for i in range(lax.axis_size(axis))])


def from_behind(value, axis, steps):
    count = lax.axis_size(axis)
    leading, last = (max(0, -steps), min(count, count - steps))
    return lax.ppermute(value, axis, [(source, source + steps) for source in range(leading, last)])


def modulated(hidden, shift_row, scale_row):
    values = hidden.astype(jnp.float32)
    centered = values - jnp.mean(values, axis=-1, keepdims=True)
    variance = jnp.mean(centered * centered, axis=-1, keepdims=True)
    normed = centered * lax.rsqrt(variance + EPSILON)
    return (normed * (1.0 + scale_row) + shift_row).astype(jnp.bfloat16)


def rms_scaled(values, gain_row):
    return (
        values * lax.rsqrt(jnp.mean(values * values, axis=-1, keepdims=True) + EPSILON) * gain_row
    )


def bit_of(value, bit):
    return (value >> bit) & 1


def block_position(group, bit_order):
    steps = len(bit_order)
    return sum(((group >> b) & 1) << (steps - 1 - k) for k, b in enumerate(bit_order))


def reduce_rows(partial, group_index, bit_order):
    current = partial
    for step, bit in enumerate(bit_order):
        middle = current.shape[0] // 2
        upper = bit_of(group_index, bit)
        kept = lax.dynamic_slice_in_dim(current, upper * middle, middle, 0)
        given = lax.dynamic_slice_in_dim(current, (1 - upper) * middle, middle, 0)
        if step > 0:
            given = given.astype(jnp.bfloat16)
        received = from_partner(given, "section", bit)
        current = kept.astype(jnp.float32) + received.astype(jnp.float32)
    return current


def gather_rows(mine, position, bit_count):
    gathered = mine
    for bit in range(bit_count):
        partner = from_partner(gathered, "section", bit)
        upper = bit_of(position, bit) == 1
        gathered = jnp.where(
            upper,
            jnp.concatenate([partner, gathered]),
            jnp.concatenate([gathered, partner]),
        )
    return gathered


def attend_all(modded, w_qkv, w_out, stale, gain_pair, tile_patch, tile_list, tile_limit, row_order):
    rows = modded.shape[0]
    tiles = rows // TILE
    ksel = tile_list.shape[1]
    head_count = w_out.shape[0] // HD
    projected = jnp.dot(modded, w_qkv, preferred_element_type=jnp.float32).reshape(
        rows, 3, head_count, HD
    )
    queries = rms_scaled(projected[:, 0], gain_pair[0]).astype(jnp.bfloat16)
    keys_new = rms_scaled(projected[:, 1], gain_pair[1]).astype(jnp.bfloat16)
    values_new = projected[:, 2].astype(jnp.bfloat16)
    fresh = jnp.concatenate(
        [keys_new.reshape(rows, head_count * HD), values_new.reshape(rows, head_count * HD)],
        axis=1,
    )
    width = fresh.shape[1]
    memory = jnp.concatenate(
        [fresh.reshape(tiles, TILE, width), stale.reshape(tiles, TILE, width)], axis=0
    )
    use_new = tile_patch[tile_list] <= tile_patch[:, None]
    picked = tile_list + jnp.where(use_new, 0, tiles)
    chosen = memory[picked]
    key_rows = chosen[..., : head_count * HD].reshape(tiles, ksel * TILE, head_count, HD)
    value_rows = chosen[..., head_count * HD :].reshape(tiles, ksel * TILE, head_count, HD)
    query_rows = queries.reshape(tiles, TILE, head_count, HD)
    scores = jnp.einsum(
        "tqhd,tkhd->thqk", query_rows, key_rows, preferred_element_type=jnp.float32
    ) / math.sqrt(HD)
    allowed = (jnp.arange(ksel * TILE) // TILE)[None, :] < tile_limit[:, None]
    scores = jnp.where(allowed[:, None, None, :], scores, -1e30)
    highest = jnp.max(scores, axis=-1, keepdims=True)
    weights = jnp.exp(scores - highest)
    probabilities = (weights / jnp.sum(weights, axis=-1, keepdims=True)).astype(jnp.bfloat16)
    attended = jnp.einsum(
        "thqk,tkhd->tqhd", probabilities, value_rows, preferred_element_type=jnp.float32
    ).astype(jnp.bfloat16)
    attended = attended.reshape(rows, head_count * HD)
    attended = row_order(attended)
    return jnp.dot(attended, w_out, preferred_element_type=jnp.float32)


def on_device(
    latent,
    control_latent,
    patch_tiles,
    tile_lists,
    tile_counts,
    embed_weight,
    control_embed,
    modulation,
    qk_gain,
    qkv_weight,
    out_weight,
    stale_cache,
    control_gain,
    final_mod,
    final_weight,
):
    section_size = lax.axis_size("section")
    slot_count = section_size // HG
    pair_count = slot_count // 2
    pair_size = 2 * HG
    device_index = lax.axis_index("section")
    slot_index = device_index // HG
    group_index = device_index % HG
    parity = slot_index % 2
    pair_index = slot_index // 2
    position = device_index % pair_size
    group_bits = HG.bit_length() - 1
    pair_bits = pair_size.bit_length() - 1

    both = jnp.concatenate([latent, control_latent], axis=1)
    whole = lax.all_gather(both, "section", axis=0, tiled=True)
    rows = whole.shape[0]
    c_out = latent.shape[1]
    tiles = rows // TILE
    final_rows = rows // pair_size
    whole_latent = whole[:, :c_out]
    whole_condition = whole[:, c_out:]
    embedded = jnp.dot(whole_latent, embed_weight, preferred_element_type=jnp.float32)
    hidden_in = embedded.astype(jnp.bfloat16)
    control_in = (
        embedded + jnp.dot(whole_condition, control_embed, preferred_element_type=jnp.float32)
    ).astype(jnp.bfloat16)

    starts = jnp.cumsum(patch_tiles) - patch_tiles
    tile_ids = jnp.arange(tiles, dtype=jnp.int32)
    tile_patch = jnp.sum((starts[None, :] <= tile_ids[:, None]).astype(jnp.int32), axis=1) - 1

    w_qkv = qkv_weight[0]
    w_out = out_weight[0]
    stale = stale_cache[0]
    shifts = modulation[slot_index]
    gain_pair = qk_gain[slot_index]
    tile_list = tile_lists[slot_index]
    tile_limit = tile_counts[slot_index]
    gate_control = modulation[2 * pair_index, 2]
    gate_main = modulation[2 * pair_index + 1, 2]
    control_row = control_gain[pair_index]

    bit_order = list(range(group_bits))
    inverse = [0] * HG
    for group in range(HG):
        inverse[block_position(group, bit_order)] = group
    halves = pair_size // HG

    def row_order(values):
        split = values.reshape(halves, HG, final_rows, values.shape[1])
        split = split[:, jnp.array(inverse)]
        return jnp.swapaxes(split, 0, 1).reshape(values.shape)

    for stage in range(pair_count):
        stream = jnp.where(parity == 0, control_in, hidden_in)
        modded = modulated(stream, shifts[0], shifts[1])
        partial = attend_all(
            modded, w_qkv, w_out, stale, gain_pair, tile_patch, tile_list, tile_limit, row_order
        ).astype(jnp.bfloat16)
        summed = reduce_rows(partial, group_index, bit_order)
        kept = lax.dynamic_slice_in_dim(summed, parity * final_rows, final_rows, 0)
        given = lax.dynamic_slice_in_dim(summed, (1 - parity) * final_rows, final_rows, 0)
        received = from_partner(given.astype(jnp.bfloat16), "section", group_bits).astype(
            jnp.float32
        )
        sum_control = jnp.where(parity == 0, kept, received)
        sum_main = jnp.where(parity == 0, received, kept)
        own_start = position * final_rows
        control_rows = lax.dynamic_slice_in_dim(control_in, own_start, final_rows, 0)
        hidden_rows = lax.dynamic_slice_in_dim(hidden_in, own_start, final_rows, 0)
        control_new = (control_rows.astype(jnp.float32) + gate_control * sum_control).astype(
            jnp.bfloat16
        )
        hidden_new = (
            hidden_rows.astype(jnp.float32)
            + gate_main * sum_main
            + control_row * control_new.astype(jnp.float32)
        ).astype(jnp.bfloat16)
        if stage + 1 < pair_count:
            moved = from_behind((control_new, hidden_new), "section", pair_size)
            control_in = gather_rows(moved[0], position, pair_bits)
            hidden_in = gather_rows(moved[1], position, pair_bits)

    denoised = jnp.dot(
        modulated(hidden_new, final_mod[0], final_mod[1]),
        final_weight,
        preferred_element_type=jnp.float32,
    )
    if pair_count == 1:
        return denoised
    is_last = pair_index == pair_count - 1
    placed = lax.dynamic_update_slice_in_dim(
        jnp.zeros((rows, denoised.shape[1]), jnp.float32),
        jnp.where(is_last, denoised, 0.0),
        position * final_rows,
        0,
    )
    return lax.psum_scatter(placed, "section", scatter_dimension=0, tiled=True)


def solution(mesh):
    return jax.shard_map(
        on_device,
        mesh=mesh,
        in_specs=(
            P(("grp", "section"), None),
            P(("grp", "section"), None),
            P(),
            P(),
            P(),
            P(),
            P(),
            P(),
            P(),
            P("section", None, None),
            P("section", None, None),
            P("section", "grp", None),
            P(),
            P(),
            P(),
        ),
        out_specs=P(("grp", "section"), None),
        check_vma=False,
    )
```

```python
import math

import jax
import jax.numpy as jnp
from jax import lax
from jax.experimental import pallas as pl
from jax.experimental.pallas import tpu as pltpu
from jax.sharding import PartitionSpec as P

HD = 128
HG = 8
TILE = 128

EPSILON = 1e-06


def from_partner(value, axis, distance):
    return lax.ppermute(value, axis, [(i, i ^ 1 << distance) for i in range(lax.axis_size(axis))])


def from_behind(value, axis, steps):
    count = lax.axis_size(axis)
    leading, last = (max(0, -steps), min(count, count - steps))
    return lax.ppermute(value, axis, [(source, source + steps) for source in range(leading, last)])


def modulated(hidden, shift_row, scale_row):
    values = hidden.astype(jnp.float32)
    centered = values - jnp.mean(values, axis=-1, keepdims=True)
    variance = jnp.mean(centered * centered, axis=-1, keepdims=True)
    normed = centered * lax.rsqrt(variance + EPSILON)
    return (normed * (1.0 + scale_row) + shift_row).astype(jnp.bfloat16)


def rms_scaled(values, gain_row):
    return (
        values * lax.rsqrt(jnp.mean(values * values, axis=-1, keepdims=True) + EPSILON) * gain_row
    )


def bit_of(value, bit):
    return (value >> bit) & 1


def gather_rows(mine, position, bit_count):
    gathered = mine
    for bit in range(bit_count):
        partner = from_partner(gathered, "section", bit)
        upper = bit_of(position, bit) == 1
        gathered = jnp.where(
            upper,
            jnp.concatenate([partner, gathered]),
            jnp.concatenate([gathered, partner]),
        )
    return gathered


def qkv_kernel(x_ref, w_ref, g_ref, o_ref):
    j = pl.program_id(0)
    acc = jnp.dot(x_ref[...], w_ref[...], preferred_element_type=jnp.float32)
    gain = g_ref[pl.ds(jnp.minimum(j, 1), 1), :]
    heads = acc.shape[1] // HD
    pieces = []
    for h in range(heads):
        values = acc[:, h * HD : (h + 1) * HD]
        scaled = values * lax.rsqrt(jnp.mean(values * values, axis=-1, keepdims=True) + EPSILON) * gain
        pieces.append(jnp.where(j < 2, scaled, values))
    o_ref[...] = jnp.concatenate(pieces, axis=1).astype(o_ref.dtype)


def project_qkv(modded, w_qkv, gain_pair):
    rows, depth = modded.shape
    width = w_qkv.shape[1] // 3
    return pl.pallas_call(
        qkv_kernel,
        out_shape=jax.ShapeDtypeStruct((rows, 3 * width), jnp.bfloat16),
        grid=(3,),
        in_specs=[
            pl.BlockSpec((rows, depth), lambda j: (0, 0)),
            pl.BlockSpec((depth, width), lambda j: (0, j)),
            pl.BlockSpec((2, HD), lambda j: (0, 0)),
        ],
        out_specs=pl.BlockSpec((rows, width), lambda j: (0, j)),
        compiler_params=pltpu.CompilerParams(vmem_limit_bytes=48 * 1024 * 1024),
        cost_estimate=pl.CostEstimate(
            flops=2 * rows * depth * 3 * width,
            bytes_accessed=2 * (rows * depth + depth * 3 * width + rows * 3 * width),
            transcendentals=0,
        ),
    )(modded, w_qkv, gain_pair)


def attention_kernel(picked_ref, limit_ref, q_ref, m0_ref, m1_ref, m2_ref, o_ref):
    t = pl.program_id(0)
    limit = limit_ref[t]
    width = q_ref.shape[1]
    heads = width // HD
    memories = (m0_ref, m1_ref, m2_ref)
    for h in range(heads):
        query = q_ref[:, h * HD : (h + 1) * HD]
        scores = []
        for j, m_ref in enumerate(memories):
            key = m_ref[:, h * HD : (h + 1) * HD]
            s = lax.dot_general(
                query, key, (((1,), (1,)), ((), ())), preferred_element_type=jnp.float32
            ) / math.sqrt(HD)
            scores.append(jnp.where(j < limit, s, -1e30))
        highest = jnp.max(scores[0], axis=-1, keepdims=True)
        for s in scores[1:]:
            highest = jnp.maximum(highest, jnp.max(s, axis=-1, keepdims=True))
        weights = [jnp.exp(s - highest) for s in scores]
        total = jnp.sum(weights[0], axis=-1, keepdims=True)
        for w in weights[1:]:
            total = total + jnp.sum(w, axis=-1, keepdims=True)
        acc = None
        for w, m_ref in zip(weights, memories):
            probabilities = (w / total).astype(jnp.bfloat16)
            value = m_ref[:, width + h * HD : width + (h + 1) * HD]
            part = jnp.dot(probabilities, value, preferred_element_type=jnp.float32)
            acc = part if acc is None else acc + part
        o_ref[:, h * HD : (h + 1) * HD] = acc.astype(o_ref.dtype)


def attend_tiles(projected, memory, picked, limit):
    rows = projected.shape[0]
    width = projected.shape[1] // 3
    tiles = rows // TILE
    mem_width = memory.shape[1]

    def memory_spec(j):
        return pl.BlockSpec((TILE, mem_width), lambda t, p, c: (p[t, j], 0))

    return pl.pallas_call(
        attention_kernel,
        out_shape=jax.ShapeDtypeStruct((rows, width), jnp.bfloat16),
        grid_spec=pltpu.PrefetchScalarGridSpec(
            num_scalar_prefetch=2,
            grid=(tiles,),
            in_specs=[
                pl.BlockSpec((TILE, width), lambda t, p, c: (t, 0)),
                memory_spec(0),
                memory_spec(1),
                memory_spec(2),
            ],
            out_specs=pl.BlockSpec((TILE, width), lambda t, p, c: (t, 0)),
        ),
        cost_estimate=pl.CostEstimate(
            flops=4 * rows * 3 * TILE * width,
            bytes_accessed=2 * (2 * rows * width + 3 * rows * mem_width),
            transcendentals=rows * 3 * TILE * (width // HD),
        ),
    )(picked, limit, projected, memory, memory, memory)


def row_table(group_count):
    table = []
    for g in range(group_count):
        first = [g, g ^ 4, g ^ 2, g ^ 6]
        second = [group_count + k for k in (g, g ^ 2, g ^ 4, g ^ 6)]
        own = first + second
        other = [g ^ 1, g ^ 5, g ^ 3, g ^ 7]
        other_second = [group_count + k for k in (g ^ 1, g ^ 3, g ^ 5, g ^ 7)]
        table.append(own + other + other_second)
    return table


def reduce_two_ways(partial):
    half = partial.shape[0] // 2
    summed = partial[:half].astype(jnp.float32) + from_partner(
        partial[half:], "section", 0
    ).astype(jnp.float32)
    quarter = half // 2
    first, second = summed[:quarter], summed[quarter:]
    eighth = quarter // 2
    first_sent = first[eighth:].astype(jnp.bfloat16)
    second_sent = second[eighth:].astype(jnp.bfloat16)
    first = first[:eighth] + from_partner(first_sent, "section", 1).astype(jnp.float32)
    second = second[:eighth] + from_partner(second_sent, "section", 2).astype(jnp.float32)
    sixteenth = eighth // 2
    first = first[:sixteenth] + from_partner(
        first[sixteenth:].astype(jnp.bfloat16), "section", 2
    ).astype(jnp.float32)
    second = second[:sixteenth] + from_partner(
        second[sixteenth:].astype(jnp.bfloat16), "section", 1
    ).astype(jnp.float32)
    return first, second


def on_device(
    latent,
    control_latent,
    patch_tiles,
    tile_lists,
    tile_counts,
    embed_weight,
    control_embed,
    modulation,
    qk_gain,
    qkv_weight,
    out_weight,
    stale_cache,
    control_gain,
    final_mod,
    final_weight,
):
    section_size = lax.axis_size("section")
    slot_count = section_size // HG
    pair_count = slot_count // 2
    pair_size = 2 * HG
    device_index = lax.axis_index("section")
    slot_index = device_index // HG
    group_index = device_index % HG
    parity = slot_index % 2
    pair_index = slot_index // 2
    position = device_index % pair_size
    group_bits = HG.bit_length() - 1
    pair_bits = pair_size.bit_length() - 1
    section_bits = section_size.bit_length() - 1

    both = jnp.concatenate([latent, control_latent], axis=1)
    whole = gather_rows(both, device_index, section_bits)
    rows = whole.shape[0]
    c_out = latent.shape[1]
    tiles = rows // TILE
    final_rows = rows // pair_size
    whole_latent = whole[:, :c_out]
    whole_condition = jnp.where(parity == 0, whole[:, c_out:], jnp.zeros_like(whole[:, c_out:]))
    embedded = jnp.dot(whole_latent, embed_weight, preferred_element_type=jnp.float32)
    stream = (
        embedded + jnp.dot(whole_condition, control_embed, preferred_element_type=jnp.float32)
    ).astype(jnp.bfloat16)
    hidden_in = embedded.astype(jnp.bfloat16)

    starts = jnp.cumsum(patch_tiles) - patch_tiles
    tile_ids = jnp.arange(tiles, dtype=jnp.int32)
    tile_patch = jnp.sum((starts[None, :] <= tile_ids[:, None]).astype(jnp.int32), axis=1) - 1

    w_qkv = qkv_weight[0]
    w_out = out_weight[0]
    stale = stale_cache[0]
    shifts = modulation[slot_index]
    gain_pair = qk_gain[slot_index]
    tile_list = tile_lists[slot_index]
    tile_limit = tile_counts[slot_index]
    use_new = tile_patch[tile_list] <= tile_patch[:, None]
    picked = (tile_list + jnp.where(use_new, 0, tiles)).astype(jnp.int32)
    gate_control = modulation[2 * pair_index, 2]
    gate_main = modulation[2 * pair_index + 1, 2]
    control_row = control_gain[pair_index]
    order = jnp.array(row_table(HG), jnp.int32)[group_index]

    for stage in range(pair_count):
        modded = modulated(stream, shifts[0], shifts[1])
        projected = project_qkv(modded, w_qkv, gain_pair)
        width = projected.shape[1] // 3
        memory = jnp.concatenate([projected[:, width:], stale], axis=0)
        attended = attend_tiles(projected, memory, picked, tile_limit.astype(jnp.int32))
        attended = attended.reshape(pair_size, final_rows, width)[order].reshape(rows, width)
        partial = jnp.dot(attended, w_out, preferred_element_type=jnp.float32).astype(
            jnp.bfloat16
        )
        first, second = reduce_two_ways(partial)
        kept = jnp.where(parity == 0, first, second)
        given = jnp.where(parity == 0, second, first)
        received = from_partner(given.astype(jnp.bfloat16), "section", group_bits).astype(
            jnp.float32
        )
        sum_control = jnp.where(parity == 0, kept, received)
        sum_main = jnp.where(parity == 0, received, kept)
        own_start = position * final_rows
        if stage == 0:
            latent_rows = lax.dynamic_slice_in_dim(whole, own_start, final_rows, 0)
            own_embedded = jnp.dot(
                latent_rows[:, :c_out], embed_weight, preferred_element_type=jnp.float32
            )
            control_rows = (
                own_embedded
                + jnp.dot(latent_rows[:, c_out:], control_embed, preferred_element_type=jnp.float32)
            ).astype(jnp.bfloat16)
            hidden_rows = own_embedded.astype(jnp.bfloat16)
        else:
            control_rows = lax.dynamic_slice_in_dim(control_in, own_start, final_rows, 0)
            hidden_rows = lax.dynamic_slice_in_dim(hidden_in, own_start, final_rows, 0)
        control_new = (control_rows.astype(jnp.float32) + gate_control * sum_control).astype(
            jnp.bfloat16
        )
        hidden_new = (
            hidden_rows.astype(jnp.float32)
            + gate_main * sum_main
            + control_row * control_new.astype(jnp.float32)
        ).astype(jnp.bfloat16)
        if stage + 1 < pair_count:
            moved = from_behind((control_new, hidden_new), "section", pair_size)
            control_in = gather_rows(moved[0], position, pair_bits)
            hidden_in = gather_rows(moved[1], position, pair_bits)
            stream = jnp.where(parity == 0, control_in, hidden_in)

    denoised = jnp.dot(
        modulated(hidden_new, final_mod[0], final_mod[1]),
        final_weight,
        preferred_element_type=jnp.float32,
    )
    if pair_count == 1:
        return denoised
    is_last = pair_index == pair_count - 1
    placed = lax.dynamic_update_slice_in_dim(
        jnp.zeros((rows, denoised.shape[1]), jnp.float32),
        jnp.where(is_last, denoised, 0.0),
        position * final_rows,
        0,
    )
    return lax.psum_scatter(placed, "section", scatter_dimension=0, tiled=True)


def solution(mesh):
    return jax.shard_map(
        on_device,
        mesh=mesh,
        in_specs=(
            P(("grp", "section"), None),
            P(("grp", "section"), None),
            P(),
            P(),
            P(),
            P(),
            P(),
            P(),
            P(),
            P("section", None, None),
            P("section", None, None),
            P("section", "grp", None),
            P(),
            P(),
            P(),
        ),
        out_specs=P(("grp", "section"), None),
        check_vma=False,
    )
```

```python
import math

import jax
import jax.numpy as jnp
from jax import lax
from jax.experimental import pallas as pl
from jax.experimental.pallas import tpu as pltpu
from jax.sharding import PartitionSpec as P

HD = 128
HG = 8
TILE = 128

EPSILON = 1e-06


def from_partner(value, axis, distance):
    return lax.ppermute(value, axis, [(i, i ^ 1 << distance) for i in range(lax.axis_size(axis))])


def from_behind(value, axis, steps):
    count = lax.axis_size(axis)
    leading, last = (max(0, -steps), min(count, count - steps))
    return lax.ppermute(value, axis, [(source, source + steps) for source in range(leading, last)])


def modulated(hidden, shift_row, scale_row):
    values = hidden.astype(jnp.float32)
    centered = values - jnp.mean(values, axis=-1, keepdims=True)
    variance = jnp.mean(centered * centered, axis=-1, keepdims=True)
    normed = centered * lax.rsqrt(variance + EPSILON)
    return (normed * (1.0 + scale_row) + shift_row).astype(jnp.bfloat16)


def rms_scaled(values, gain_row):
    return (
        values * lax.rsqrt(jnp.mean(values * values, axis=-1, keepdims=True) + EPSILON) * gain_row
    )


def bit_of(value, bit):
    return (value >> bit) & 1


def gather_rows(mine, position, bit_count):
    gathered = mine
    for bit in range(bit_count):
        partner = from_partner(gathered, "section", bit)
        upper = bit_of(position, bit) == 1
        gathered = jnp.where(
            upper,
            jnp.concatenate([partner, gathered]),
            jnp.concatenate([gathered, partner]),
        )
    return gathered


def qkv_kernel(x_ref, w_ref, g_ref, o_ref):
    j = pl.program_id(0)
    acc = jnp.dot(x_ref[...], w_ref[...], preferred_element_type=jnp.float32)
    gain = g_ref[pl.ds(jnp.minimum(j, 1), 1), :]
    heads = acc.shape[1] // HD
    pieces = []
    for h in range(heads):
        values = acc[:, h * HD : (h + 1) * HD]
        scaled = values * lax.rsqrt(jnp.mean(values * values, axis=-1, keepdims=True) + EPSILON) * gain
        pieces.append(jnp.where(j < 2, scaled, values))
    o_ref[...] = jnp.concatenate(pieces, axis=1).astype(o_ref.dtype)


def project_qkv(modded, w_qkv, gain_pair):
    rows, depth = modded.shape
    width = w_qkv.shape[1] // 3
    return pl.pallas_call(
        qkv_kernel,
        out_shape=jax.ShapeDtypeStruct((rows, 3 * width), jnp.bfloat16),
        grid=(3,),
        in_specs=[
            pl.BlockSpec((rows, depth), lambda j: (0, 0)),
            pl.BlockSpec((depth, width), lambda j: (0, j)),
            pl.BlockSpec((2, HD), lambda j: (0, 0)),
        ],
        out_specs=pl.BlockSpec((rows, width), lambda j: (0, j)),
        compiler_params=pltpu.CompilerParams(vmem_limit_bytes=48 * 1024 * 1024),
        cost_estimate=pl.CostEstimate(
            flops=2 * rows * depth * 3 * width,
            bytes_accessed=2 * (rows * depth + depth * 3 * width + rows * 3 * width),
            transcendentals=0,
        ),
    )(modded, w_qkv, gain_pair)


def attention_kernel(picked_ref, limit_ref, q_ref, m0_ref, m1_ref, m2_ref, o_ref):
    t = pl.program_id(0)
    limit = limit_ref[t]
    width = q_ref.shape[1]
    heads = width // HD
    memories = (m0_ref, m1_ref, m2_ref)
    tile_rows = m0_ref.shape[0]
    key_tile = lax.broadcasted_iota(jnp.int32, (1, len(memories) * tile_rows), 1) // tile_rows
    allowed = key_tile < limit
    for h in range(heads):
        query = q_ref[:, h * HD : (h + 1) * HD]
        keys = jnp.concatenate([m[:, h * HD : (h + 1) * HD] for m in memories], axis=0)
        values = jnp.concatenate(
            [m[:, width + h * HD : width + (h + 1) * HD] for m in memories], axis=0
        )
        scores = lax.dot_general(
            query, keys, (((1,), (1,)), ((), ())), preferred_element_type=jnp.float32
        ) / math.sqrt(HD)
        scores = jnp.where(allowed, scores, -1e30)
        highest = jnp.max(scores, axis=-1, keepdims=True)
        weights = jnp.exp(scores - highest)
        probabilities = (weights / jnp.sum(weights, axis=-1, keepdims=True)).astype(jnp.bfloat16)
        acc = jnp.dot(probabilities, values, preferred_element_type=jnp.float32)
        o_ref[:, h * HD : (h + 1) * HD] = acc.astype(o_ref.dtype)

def gather_all(mine, index, count):
    blocks = [mine]
    for shift in range(1, count):
        blocks.append(
            lax.ppermute(mine, "section", [(i, (i + shift) % count) for i in range(count)])
        )
    stacked = jnp.stack(blocks)
    sources = (index - jnp.arange(count)) % count
    return stacked[sources].reshape((count * mine.shape[0],) + mine.shape[1:])


def attend_tiles(projected, memory, picked, limit):
    rows = projected.shape[0]
    width = projected.shape[1] // 3
    tiles = rows // TILE
    mem_width = memory.shape[1]

    def memory_spec(j):
        return pl.BlockSpec((TILE, mem_width), lambda t, p, c: (p[t, j], 0))

    return pl.pallas_call(
        attention_kernel,
        out_shape=jax.ShapeDtypeStruct((rows, width), jnp.bfloat16),
        grid_spec=pltpu.PrefetchScalarGridSpec(
            num_scalar_prefetch=2,
            grid=(tiles,),
            in_specs=[
                pl.BlockSpec((TILE, width), lambda t, p, c: (t, 0)),
                memory_spec(0),
                memory_spec(1),
                memory_spec(2),
            ],
            out_specs=pl.BlockSpec((TILE, width), lambda t, p, c: (t, 0)),
        ),
        cost_estimate=pl.CostEstimate(
            flops=4 * rows * 3 * TILE * width,
            bytes_accessed=2 * (2 * rows * width + 3 * rows * mem_width),
            transcendentals=rows * 3 * TILE * (width // HD),
        ),
    )(picked, limit, projected, memory, memory, memory)


def row_table(group_count):
    table = []
    for g in range(group_count):
        first = [g, g ^ 4, g ^ 2, g ^ 6]
        second = [group_count + k for k in (g, g ^ 2, g ^ 4, g ^ 6)]
        own = first + second
        other = [g ^ 1, g ^ 5, g ^ 3, g ^ 7]
        other_second = [group_count + k for k in (g ^ 1, g ^ 3, g ^ 5, g ^ 7)]
        table.append(own + other + other_second)
    return table


def reduce_two_ways(partial):
    half = partial.shape[0] // 2
    summed = partial[:half].astype(jnp.float32) + from_partner(
        partial[half:], "section", 0
    ).astype(jnp.float32)
    quarter = half // 2
    first, second = summed[:quarter], summed[quarter:]
    eighth = quarter // 2
    first_sent = first[eighth:].astype(jnp.bfloat16)
    second_sent = second[eighth:].astype(jnp.bfloat16)
    first = first[:eighth] + from_partner(first_sent, "section", 1).astype(jnp.float32)
    second = second[:eighth] + from_partner(second_sent, "section", 2).astype(jnp.float32)
    sixteenth = eighth // 2
    first = first[:sixteenth] + from_partner(
        first[sixteenth:].astype(jnp.bfloat16), "section", 2
    ).astype(jnp.float32)
    second = second[:sixteenth] + from_partner(
        second[sixteenth:].astype(jnp.bfloat16), "section", 1
    ).astype(jnp.float32)
    return first, second


def on_device(
    latent,
    control_latent,
    patch_tiles,
    tile_lists,
    tile_counts,
    embed_weight,
    control_embed,
    modulation,
    qk_gain,
    qkv_weight,
    out_weight,
    stale_cache,
    control_gain,
    final_mod,
    final_weight,
):
    section_size = lax.axis_size("section")
    slot_count = section_size // HG
    pair_count = slot_count // 2
    pair_size = 2 * HG
    device_index = lax.axis_index("section")
    slot_index = device_index // HG
    group_index = device_index % HG
    parity = slot_index % 2
    pair_index = slot_index // 2
    position = device_index % pair_size
    group_bits = HG.bit_length() - 1
    pair_bits = pair_size.bit_length() - 1
    section_bits = section_size.bit_length() - 1

    both = jnp.concatenate([latent, control_latent], axis=1)
    whole = gather_all(both, device_index, section_size)
    rows = whole.shape[0]
    c_out = latent.shape[1]
    tiles = rows // TILE
    final_rows = rows // pair_size
    whole_latent = whole[:, :c_out]
    whole_condition = jnp.where(parity == 0, whole[:, c_out:], jnp.zeros_like(whole[:, c_out:]))
    embedded = jnp.dot(whole_latent, embed_weight, preferred_element_type=jnp.float32)
    stream = (
        embedded + jnp.dot(whole_condition, control_embed, preferred_element_type=jnp.float32)
    ).astype(jnp.bfloat16)
    hidden_in = embedded.astype(jnp.bfloat16)

    starts = jnp.cumsum(patch_tiles) - patch_tiles
    tile_ids = jnp.arange(tiles, dtype=jnp.int32)
    tile_patch = jnp.sum((starts[None, :] <= tile_ids[:, None]).astype(jnp.int32), axis=1) - 1

    w_qkv = qkv_weight[0]
    w_out = out_weight[0]
    stale = stale_cache[0]
    shifts = modulation[slot_index]
    gain_pair = qk_gain[slot_index]
    tile_list = tile_lists[slot_index]
    tile_limit = tile_counts[slot_index]
    use_new = tile_patch[tile_list] <= tile_patch[:, None]
    picked = (tile_list + jnp.where(use_new, 0, tiles)).astype(jnp.int32)
    gate_control = modulation[2 * pair_index, 2]
    gate_main = modulation[2 * pair_index + 1, 2]
    control_row = control_gain[pair_index]
    order = jnp.array(row_table(HG), jnp.int32)[group_index]

    for stage in range(pair_count):
        modded = modulated(stream, shifts[0], shifts[1])
        projected = project_qkv(modded, w_qkv, gain_pair)
        width = projected.shape[1] // 3
        memory = jnp.concatenate([projected[:, width:], stale], axis=0)
        attended = attend_tiles(projected, memory, picked, tile_limit.astype(jnp.int32))
        attended = attended.reshape(pair_size, final_rows, width)[order].reshape(rows, width)
        partial = jnp.dot(attended, w_out, preferred_element_type=jnp.float32).astype(
            jnp.bfloat16
        )
        first, second = reduce_two_ways(partial)
        kept = jnp.where(parity == 0, first, second)
        given = jnp.where(parity == 0, second, first)
        received = from_partner(given.astype(jnp.bfloat16), "section", group_bits).astype(
            jnp.float32
        )
        sum_control = jnp.where(parity == 0, kept, received)
        sum_main = jnp.where(parity == 0, received, kept)
        own_start = position * final_rows
        if stage == 0:
            latent_rows = lax.dynamic_slice_in_dim(whole, own_start, final_rows, 0)
            own_embedded = jnp.dot(
                latent_rows[:, :c_out], embed_weight, preferred_element_type=jnp.float32
            )
            control_rows = (
                own_embedded
                + jnp.dot(latent_rows[:, c_out:], control_embed, preferred_element_type=jnp.float32)
            ).astype(jnp.bfloat16)
            hidden_rows = own_embedded.astype(jnp.bfloat16)
        else:
            control_rows = lax.dynamic_slice_in_dim(control_in, own_start, final_rows, 0)
            hidden_rows = lax.dynamic_slice_in_dim(hidden_in, own_start, final_rows, 0)
        control_new = (control_rows.astype(jnp.float32) + gate_control * sum_control).astype(
            jnp.bfloat16
        )
        hidden_new = (
            hidden_rows.astype(jnp.float32)
            + gate_main * sum_main
            + control_row * control_new.astype(jnp.float32)
        ).astype(jnp.bfloat16)
        if stage + 1 < pair_count:
            moved = from_behind((control_new, hidden_new), "section", pair_size)
            control_in = gather_rows(moved[0], position, pair_bits)
            hidden_in = gather_rows(moved[1], position, pair_bits)
            stream = jnp.where(parity == 0, control_in, hidden_in)

    denoised = jnp.dot(
        modulated(hidden_new, final_mod[0], final_mod[1]),
        final_weight,
        preferred_element_type=jnp.float32,
    )
    if pair_count == 1:
        return denoised
    is_last = pair_index == pair_count - 1
    placed = lax.dynamic_update_slice_in_dim(
        jnp.zeros((rows, denoised.shape[1]), jnp.float32),
        jnp.where(is_last, denoised, 0.0),
        position * final_rows,
        0,
    )
    return lax.psum_scatter(placed, "section", scatter_dimension=0, tiled=True)


def solution(mesh):
    return jax.shard_map(
        on_device,
        mesh=mesh,
        in_specs=(
            P(("grp", "section"), None),
            P(("grp", "section"), None),
            P(),
            P(),
            P(),
            P(),
            P(),
            P(),
            P(),
            P("section", None, None),
            P("section", None, None),
            P("section", "grp", None),
            P(),
            P(),
            P(),
        ),
        out_specs=P(("grp", "section"), None),
        check_vma=False,
    )
```

```python
import math

import jax
import jax.numpy as jnp
from jax import lax
from jax.experimental import pallas as pl
from jax.experimental.pallas import tpu as pltpu
from jax.sharding import PartitionSpec as P

HD = 128
HG = 8
TILE = 128

EPSILON = 1e-06


def from_partner(value, axis, distance):
    return lax.ppermute(value, axis, [(i, i ^ 1 << distance) for i in range(lax.axis_size(axis))])


def from_behind(value, axis, steps):
    count = lax.axis_size(axis)
    leading, last = (max(0, -steps), min(count, count - steps))
    return lax.ppermute(value, axis, [(source, source + steps) for source in range(leading, last)])


def modulated(hidden, shift_row, scale_row):
    values = hidden.astype(jnp.float32)
    centered = values - jnp.mean(values, axis=-1, keepdims=True)
    variance = jnp.mean(centered * centered, axis=-1, keepdims=True)
    normed = centered * lax.rsqrt(variance + EPSILON)
    return (normed * (1.0 + scale_row) + shift_row).astype(jnp.bfloat16)


def rms_scaled(values, gain_row):
    return (
        values * lax.rsqrt(jnp.mean(values * values, axis=-1, keepdims=True) + EPSILON) * gain_row
    )


def bit_of(value, bit):
    return (value >> bit) & 1


def gather_rows(mine, position, bit_count):
    gathered = mine
    for bit in range(bit_count):
        partner = from_partner(gathered, "section", bit)
        upper = bit_of(position, bit) == 1
        gathered = jnp.where(
            upper,
            jnp.concatenate([partner, gathered]),
            jnp.concatenate([gathered, partner]),
        )
    return gathered


def qkv_kernel(x_ref, w_ref, g_ref, o_ref):
    j = pl.program_id(0)
    acc = jnp.dot(x_ref[...], w_ref[...], preferred_element_type=jnp.float32)
    gain = g_ref[pl.ds(jnp.minimum(j, 1), 1), :]
    heads = acc.shape[1] // HD
    pieces = []
    for h in range(heads):
        values = acc[:, h * HD : (h + 1) * HD]
        scaled = values * lax.rsqrt(jnp.mean(values * values, axis=-1, keepdims=True) + EPSILON) * gain
        pieces.append(jnp.where(j < 2, scaled, values))
    o_ref[...] = jnp.concatenate(pieces, axis=1).astype(o_ref.dtype)


def project_qkv(modded, w_qkv, gain_pair):
    rows, depth = modded.shape
    width = w_qkv.shape[1] // 3
    return pl.pallas_call(
        qkv_kernel,
        out_shape=jax.ShapeDtypeStruct((rows, 3 * width), jnp.bfloat16),
        grid=(3,),
        in_specs=[
            pl.BlockSpec((rows, depth), lambda j: (0, 0)),
            pl.BlockSpec((depth, width), lambda j: (0, j)),
            pl.BlockSpec((2, HD), lambda j: (0, 0)),
        ],
        out_specs=pl.BlockSpec((rows, width), lambda j: (0, j)),
        compiler_params=pltpu.CompilerParams(vmem_limit_bytes=48 * 1024 * 1024),
        cost_estimate=pl.CostEstimate(
            flops=2 * rows * depth * 3 * width,
            bytes_accessed=2 * (rows * depth + depth * 3 * width + rows * 3 * width),
            transcendentals=0,
        ),
    )(modded, w_qkv, gain_pair)


def attention_kernel(picked_ref, limit_ref, q_ref, m0_ref, m1_ref, m2_ref, o_ref):
    t = pl.program_id(0)
    limit = limit_ref[t]
    width = q_ref.shape[1]
    heads = width // HD
    memories = (m0_ref, m1_ref, m2_ref)
    tile_rows = m0_ref.shape[0]
    key_tile = lax.broadcasted_iota(jnp.int32, (1, len(memories) * tile_rows), 1) // tile_rows
    allowed = key_tile < limit
    for h in range(heads):
        query = q_ref[:, h * HD : (h + 1) * HD]
        keys = jnp.concatenate([m[:, h * HD : (h + 1) * HD] for m in memories], axis=0)
        values = jnp.concatenate(
            [m[:, width + h * HD : width + (h + 1) * HD] for m in memories], axis=0
        )
        scores = lax.dot_general(
            query, keys, (((1,), (1,)), ((), ())), preferred_element_type=jnp.float32
        ) / math.sqrt(HD)
        scores = jnp.where(allowed, scores, -1e30)
        highest = jnp.max(scores, axis=-1, keepdims=True)
        weights = jnp.exp(scores - highest)
        probabilities = (weights / jnp.sum(weights, axis=-1, keepdims=True)).astype(jnp.bfloat16)
        acc = jnp.dot(probabilities, values, preferred_element_type=jnp.float32)
        o_ref[:, h * HD : (h + 1) * HD] = acc.astype(o_ref.dtype)

def gather_all(mine, index, count):
    spread = jnp.broadcast_to(mine[None], (count,) + mine.shape)
    gathered = lax.all_to_all(spread, "section", 0, 0, tiled=False)
    return gathered.reshape((count * mine.shape[0],) + mine.shape[1:])

def attend_tiles(projected, memory, picked, limit):
    rows = projected.shape[0]
    width = projected.shape[1] // 3
    tiles = rows // TILE
    mem_width = memory.shape[1]

    def memory_spec(j):
        return pl.BlockSpec((TILE, mem_width), lambda t, p, c: (p[t, j], 0))

    return pl.pallas_call(
        attention_kernel,
        out_shape=jax.ShapeDtypeStruct((rows, width), jnp.bfloat16),
        grid_spec=pltpu.PrefetchScalarGridSpec(
            num_scalar_prefetch=2,
            grid=(tiles,),
            in_specs=[
                pl.BlockSpec((TILE, width), lambda t, p, c: (t, 0)),
                memory_spec(0),
                memory_spec(1),
                memory_spec(2),
            ],
            out_specs=pl.BlockSpec((TILE, width), lambda t, p, c: (t, 0)),
        ),
        cost_estimate=pl.CostEstimate(
            flops=4 * rows * 3 * TILE * width,
            bytes_accessed=2 * (2 * rows * width + 3 * rows * mem_width),
            transcendentals=rows * 3 * TILE * (width // HD),
        ),
    )(picked, limit, projected, memory, memory, memory)


def row_table(group_count):
    table = []
    for g in range(group_count):
        first = [g, g ^ 4, g ^ 2, g ^ 6]
        second = [group_count + k for k in (g, g ^ 2, g ^ 4, g ^ 6)]
        own = first + second
        other = [g ^ 1, g ^ 5, g ^ 3, g ^ 7]
        other_second = [group_count + k for k in (g ^ 1, g ^ 3, g ^ 5, g ^ 7)]
        table.append(own + other + other_second)
    return table


def reduce_two_ways(partial):
    half = partial.shape[0] // 2
    summed = partial[:half].astype(jnp.float32) + from_partner(
        partial[half:], "section", 0
    ).astype(jnp.float32)
    quarter = half // 2
    first, second = summed[:quarter], summed[quarter:]
    eighth = quarter // 2
    first_sent = first[eighth:].astype(jnp.bfloat16)
    second_sent = second[eighth:].astype(jnp.bfloat16)
    first = first[:eighth] + from_partner(first_sent, "section", 1).astype(jnp.float32)
    second = second[:eighth] + from_partner(second_sent, "section", 2).astype(jnp.float32)
    sixteenth = eighth // 2
    first = first[:sixteenth] + from_partner(
        first[sixteenth:].astype(jnp.bfloat16), "section", 2
    ).astype(jnp.float32)
    second = second[:sixteenth] + from_partner(
        second[sixteenth:].astype(jnp.bfloat16), "section", 1
    ).astype(jnp.float32)
    return first, second


def on_device(
    latent,
    control_latent,
    patch_tiles,
    tile_lists,
    tile_counts,
    embed_weight,
    control_embed,
    modulation,
    qk_gain,
    qkv_weight,
    out_weight,
    stale_cache,
    control_gain,
    final_mod,
    final_weight,
):
    section_size = lax.axis_size("section")
    slot_count = section_size // HG
    pair_count = slot_count // 2
    pair_size = 2 * HG
    device_index = lax.axis_index("section")
    slot_index = device_index // HG
    group_index = device_index % HG
    parity = slot_index % 2
    pair_index = slot_index // 2
    position = device_index % pair_size
    group_bits = HG.bit_length() - 1
    pair_bits = pair_size.bit_length() - 1
    section_bits = section_size.bit_length() - 1

    both = jnp.concatenate([latent, control_latent], axis=1)
    whole = gather_all(both, device_index, section_size)
    rows = whole.shape[0]
    c_out = latent.shape[1]
    tiles = rows // TILE
    final_rows = rows // pair_size
    whole_latent = whole[:, :c_out]
    whole_condition = jnp.where(parity == 0, whole[:, c_out:], jnp.zeros_like(whole[:, c_out:]))
    embedded = jnp.dot(whole_latent, embed_weight, preferred_element_type=jnp.float32)
    stream = (
        embedded + jnp.dot(whole_condition, control_embed, preferred_element_type=jnp.float32)
    ).astype(jnp.bfloat16)
    hidden_in = embedded.astype(jnp.bfloat16)

    starts = jnp.cumsum(patch_tiles) - patch_tiles
    tile_ids = jnp.arange(tiles, dtype=jnp.int32)
    tile_patch = jnp.sum((starts[None, :] <= tile_ids[:, None]).astype(jnp.int32), axis=1) - 1

    w_qkv = qkv_weight[0]
    w_out = out_weight[0]
    stale = stale_cache[0]
    shifts = modulation[slot_index]
    gain_pair = qk_gain[slot_index]
    tile_list = tile_lists[slot_index]
    tile_limit = tile_counts[slot_index]
    use_new = tile_patch[tile_list] <= tile_patch[:, None]
    picked = (tile_list + jnp.where(use_new, 0, tiles)).astype(jnp.int32)
    gate_control = modulation[2 * pair_index, 2]
    gate_main = modulation[2 * pair_index + 1, 2]
    control_row = control_gain[pair_index]
    order = jnp.array(row_table(HG), jnp.int32)[group_index]

    for stage in range(pair_count):
        modded = modulated(stream, shifts[0], shifts[1])
        projected = project_qkv(modded, w_qkv, gain_pair)
        width = projected.shape[1] // 3
        memory = jnp.concatenate([projected[:, width:], stale], axis=0)
        attended = attend_tiles(projected, memory, picked, tile_limit.astype(jnp.int32))
        attended = attended.reshape(pair_size, final_rows, width)[order].reshape(rows, width)
        partial = jnp.dot(attended, w_out, preferred_element_type=jnp.float32).astype(
            jnp.bfloat16
        )
        first, second = reduce_two_ways(partial)
        kept = jnp.where(parity == 0, first, second)
        given = jnp.where(parity == 0, second, first)
        received = from_partner(given.astype(jnp.bfloat16), "section", group_bits).astype(
            jnp.float32
        )
        sum_control = jnp.where(parity == 0, kept, received)
        sum_main = jnp.where(parity == 0, received, kept)
        own_start = position * final_rows
        if stage == 0:
            latent_rows = lax.dynamic_slice_in_dim(whole, own_start, final_rows, 0)
            own_embedded = jnp.dot(
                latent_rows[:, :c_out], embed_weight, preferred_element_type=jnp.float32
            )
            control_rows = (
                own_embedded
                + jnp.dot(latent_rows[:, c_out:], control_embed, preferred_element_type=jnp.float32)
            ).astype(jnp.bfloat16)
            hidden_rows = own_embedded.astype(jnp.bfloat16)
        else:
            control_rows = lax.dynamic_slice_in_dim(control_in, own_start, final_rows, 0)
            hidden_rows = lax.dynamic_slice_in_dim(hidden_in, own_start, final_rows, 0)
        control_new = (control_rows.astype(jnp.float32) + gate_control * sum_control).astype(
            jnp.bfloat16
        )
        hidden_new = (
            hidden_rows.astype(jnp.float32)
            + gate_main * sum_main
            + control_row * control_new.astype(jnp.float32)
        ).astype(jnp.bfloat16)
        if stage + 1 < pair_count:
            moved = from_behind((control_new, hidden_new), "section", pair_size)
            control_in = gather_rows(moved[0], position, pair_bits)
            hidden_in = gather_rows(moved[1], position, pair_bits)
            stream = jnp.where(parity == 0, control_in, hidden_in)

    denoised = jnp.dot(
        modulated(hidden_new, final_mod[0], final_mod[1]),
        final_weight,
        preferred_element_type=jnp.float32,
    )
    if pair_count == 1:
        return denoised
    is_last = pair_index == pair_count - 1
    placed = lax.dynamic_update_slice_in_dim(
        jnp.zeros((rows, denoised.shape[1]), jnp.float32),
        jnp.where(is_last, denoised, 0.0),
        position * final_rows,
        0,
    )
    return lax.psum_scatter(placed, "section", scatter_dimension=0, tiled=True)


def solution(mesh):
    return jax.shard_map(
        on_device,
        mesh=mesh,
        in_specs=(
            P(("grp", "section"), None),
            P(("grp", "section"), None),
            P(),
            P(),
            P(),
            P(),
            P(),
            P(),
            P(),
            P("section", None, None),
            P("section", None, None),
            P("section", "grp", None),
            P(),
            P(),
            P(),
        ),
        out_specs=P(("grp", "section"), None),
        check_vma=False,
    )
```

```python
import math

import jax
import jax.numpy as jnp
from jax import lax
from jax.experimental import pallas as pl
from jax.experimental.pallas import tpu as pltpu
from jax.sharding import PartitionSpec as P

HD = 128
HG = 8
TILE = 128

EPSILON = 1e-06


def from_partner(value, axis, distance):
    return lax.ppermute(value, axis, [(i, i ^ 1 << distance) for i in range(lax.axis_size(axis))])


def from_behind(value, axis, steps):
    count = lax.axis_size(axis)
    leading, last = (max(0, -steps), min(count, count - steps))
    return lax.ppermute(value, axis, [(source, source + steps) for source in range(leading, last)])


def modulated(hidden, shift_row, scale_row):
    values = hidden.astype(jnp.float32)
    centered = values - jnp.mean(values, axis=-1, keepdims=True)
    variance = jnp.mean(centered * centered, axis=-1, keepdims=True)
    normed = centered * lax.rsqrt(variance + EPSILON)
    return (normed * (1.0 + scale_row) + shift_row).astype(jnp.bfloat16)


def rms_scaled(values, gain_row):
    return (
        values * lax.rsqrt(jnp.mean(values * values, axis=-1, keepdims=True) + EPSILON) * gain_row
    )


def bit_of(value, bit):
    return (value >> bit) & 1


def gather_rows(mine, position, bit_count):
    gathered = mine
    for bit in range(bit_count):
        partner = from_partner(gathered, "section", bit)
        upper = bit_of(position, bit) == 1
        gathered = jnp.where(
            upper,
            jnp.concatenate([partner, gathered]),
            jnp.concatenate([gathered, partner]),
        )
    return gathered


def qkv_kernel(x_ref, w_ref, g_ref, m_ref, o_ref, n_ref):
    j = pl.program_id(0)
    chunk = 64

    @pl.when(j == 0)
    def _():
        shift = m_ref[0:1, :]
        scale = 1.0 + m_ref[1:2, :]

        def body(i, carry):
            r = pl.ds(pl.multiple_of(i * chunk, chunk), chunk)
            values = x_ref[r, :].astype(jnp.float32)
            centered = values - jnp.mean(values, axis=-1, keepdims=True)
            variance = jnp.mean(centered * centered, axis=-1, keepdims=True)
            normed = centered * lax.rsqrt(variance + EPSILON)
            n_ref[r, :] = (normed * scale + shift).astype(n_ref.dtype)
            return carry

        lax.fori_loop(0, x_ref.shape[0] // chunk, body, 0)

    acc = jnp.dot(n_ref[...], w_ref[...], preferred_element_type=jnp.float32)
    gain = g_ref[pl.ds(jnp.minimum(j, 1), 1), :]
    heads = acc.shape[1] // HD
    pieces = []
    for h in range(heads):
        values = acc[:, h * HD : (h + 1) * HD]
        scaled = values * lax.rsqrt(jnp.mean(values * values, axis=-1, keepdims=True) + EPSILON) * gain
        pieces.append(jnp.where(j < 2, scaled, values))
    o_ref[...] = jnp.concatenate(pieces, axis=1).astype(o_ref.dtype)


def project_qkv(stream, w_qkv, gain_pair, shift_scale):
    rows, depth = stream.shape
    width = w_qkv.shape[1] // 3
    return pl.pallas_call(
        qkv_kernel,
        out_shape=jax.ShapeDtypeStruct((rows, 3 * width), jnp.bfloat16),
        grid=(3,),
        in_specs=[
            pl.BlockSpec((rows, depth), lambda j: (0, 0)),
            pl.BlockSpec((depth, width), lambda j: (0, j)),
            pl.BlockSpec((2, HD), lambda j: (0, 0)),
            pl.BlockSpec((2, depth), lambda j: (0, 0)),
        ],
        out_specs=pl.BlockSpec((rows, width), lambda j: (0, j)),
        scratch_shapes=[pltpu.VMEM((rows, depth), jnp.bfloat16)],
        compiler_params=pltpu.CompilerParams(
            dimension_semantics=("arbitrary",), vmem_limit_bytes=48 * 1024 * 1024
        ),
        cost_estimate=pl.CostEstimate(
            flops=2 * rows * depth * 3 * width,
            bytes_accessed=2 * (rows * depth + depth * 3 * width + rows * 3 * width),
            transcendentals=0,
        ),
    )(stream, w_qkv, gain_pair, shift_scale)

def attention_kernel(picked_ref, limit_ref, q_ref, m0_ref, m1_ref, m2_ref, o_ref):
    t = pl.program_id(0)
    limit = limit_ref[t]
    width = q_ref.shape[1]
    heads = width // HD
    memories = (m0_ref, m1_ref, m2_ref)
    tile_rows = m0_ref.shape[0]
    key_tile = lax.broadcasted_iota(jnp.int32, (1, len(memories) * tile_rows), 1) // tile_rows
    allowed = key_tile < limit
    for h in range(heads):
        query = q_ref[:, h * HD : (h + 1) * HD]
        keys = jnp.concatenate([m[:, h * HD : (h + 1) * HD] for m in memories], axis=0)
        values = jnp.concatenate(
            [m[:, width + h * HD : width + (h + 1) * HD] for m in memories], axis=0
        )
        scores = lax.dot_general(
            query, keys, (((1,), (1,)), ((), ())), preferred_element_type=jnp.float32
        ) / math.sqrt(HD)
        scores = jnp.where(allowed, scores, -1e30)
        highest = jnp.max(scores, axis=-1, keepdims=True)
        weights = jnp.exp(scores - highest)
        probabilities = (weights / jnp.sum(weights, axis=-1, keepdims=True)).astype(jnp.bfloat16)
        acc = jnp.dot(probabilities, values, preferred_element_type=jnp.float32)
        o_ref[:, h * HD : (h + 1) * HD] = acc.astype(o_ref.dtype)

def gather_all(mine, index, count):
    spread = jnp.broadcast_to(mine[None], (count,) + mine.shape)
    gathered = lax.all_to_all(spread, "section", 0, 0, tiled=False)
    return gathered.reshape((count * mine.shape[0],) + mine.shape[1:])

def attend_tiles(projected, memory, picked, limit):
    rows = projected.shape[0]
    width = projected.shape[1] // 3
    tiles = rows // TILE
    mem_width = memory.shape[1]

    def memory_spec(j):
        return pl.BlockSpec((TILE, mem_width), lambda t, p, c: (p[t, j], 0))

    return pl.pallas_call(
        attention_kernel,
        out_shape=jax.ShapeDtypeStruct((rows, width), jnp.bfloat16),
        grid_spec=pltpu.PrefetchScalarGridSpec(
            num_scalar_prefetch=2,
            grid=(tiles,),
            in_specs=[
                pl.BlockSpec((TILE, width), lambda t, p, c: (t, 0)),
                memory_spec(0),
                memory_spec(1),
                memory_spec(2),
            ],
            out_specs=pl.BlockSpec((TILE, width), lambda t, p, c: (t, 0)),
        ),
        cost_estimate=pl.CostEstimate(
            flops=4 * rows * 3 * TILE * width,
            bytes_accessed=2 * (2 * rows * width + 3 * rows * mem_width),
            transcendentals=rows * 3 * TILE * (width // HD),
        ),
    )(picked, limit, projected, memory, memory, memory)


def row_table(group_count):
    table = []
    for g in range(group_count):
        first = [g, g ^ 4, g ^ 2, g ^ 6]
        second = [group_count + k for k in (g, g ^ 2, g ^ 4, g ^ 6)]
        own = first + second
        other = [g ^ 1, g ^ 5, g ^ 3, g ^ 7]
        other_second = [group_count + k for k in (g ^ 1, g ^ 3, g ^ 5, g ^ 7)]
        table.append(own + other + other_second)
    return table


def reduce_two_ways(partial):
    half = partial.shape[0] // 2
    summed = partial[:half].astype(jnp.float32) + from_partner(
        partial[half:], "section", 0
    ).astype(jnp.float32)
    quarter = half // 2
    first, second = summed[:quarter], summed[quarter:]
    eighth = quarter // 2
    first_sent = first[eighth:].astype(jnp.bfloat16)
    second_sent = second[eighth:].astype(jnp.bfloat16)
    first = first[:eighth] + from_partner(first_sent, "section", 1).astype(jnp.float32)
    second = second[:eighth] + from_partner(second_sent, "section", 2).astype(jnp.float32)
    sixteenth = eighth // 2
    first = first[:sixteenth] + from_partner(
        first[sixteenth:].astype(jnp.bfloat16), "section", 2
    ).astype(jnp.float32)
    second = second[:sixteenth] + from_partner(
        second[sixteenth:].astype(jnp.bfloat16), "section", 1
    ).astype(jnp.float32)
    return first, second


def on_device(
    latent,
    control_latent,
    patch_tiles,
    tile_lists,
    tile_counts,
    embed_weight,
    control_embed,
    modulation,
    qk_gain,
    qkv_weight,
    out_weight,
    stale_cache,
    control_gain,
    final_mod,
    final_weight,
):
    section_size = lax.axis_size("section")
    slot_count = section_size // HG
    pair_count = slot_count // 2
    pair_size = 2 * HG
    device_index = lax.axis_index("section")
    slot_index = device_index // HG
    group_index = device_index % HG
    parity = slot_index % 2
    pair_index = slot_index // 2
    position = device_index % pair_size
    group_bits = HG.bit_length() - 1
    pair_bits = pair_size.bit_length() - 1
    section_bits = section_size.bit_length() - 1

    both = jnp.concatenate([latent, control_latent], axis=1)
    whole = gather_all(both, device_index, section_size)
    rows = whole.shape[0]
    c_out = latent.shape[1]
    tiles = rows // TILE
    final_rows = rows // pair_size
    whole_latent = whole[:, :c_out]
    whole_condition = jnp.where(parity == 0, whole[:, c_out:], jnp.zeros_like(whole[:, c_out:]))
    embedded = jnp.dot(whole_latent, embed_weight, preferred_element_type=jnp.float32)
    stream = (
        embedded + jnp.dot(whole_condition, control_embed, preferred_element_type=jnp.float32)
    ).astype(jnp.bfloat16)
    hidden_in = embedded.astype(jnp.bfloat16)

    starts = jnp.cumsum(patch_tiles) - patch_tiles
    tile_ids = jnp.arange(tiles, dtype=jnp.int32)
    tile_patch = jnp.sum((starts[None, :] <= tile_ids[:, None]).astype(jnp.int32), axis=1) - 1

    w_qkv = qkv_weight[0]
    w_out = out_weight[0]
    stale = stale_cache[0]
    shifts = modulation[slot_index]
    gain_pair = qk_gain[slot_index]
    tile_list = tile_lists[slot_index]
    tile_limit = tile_counts[slot_index]
    use_new = tile_patch[tile_list] <= tile_patch[:, None]
    picked = (tile_list + jnp.where(use_new, 0, tiles)).astype(jnp.int32)
    gate_control = modulation[2 * pair_index, 2]
    gate_main = modulation[2 * pair_index + 1, 2]
    control_row = control_gain[pair_index]
    order = jnp.array(row_table(HG), jnp.int32)[group_index]

    for stage in range(pair_count):
        projected = project_qkv(stream, w_qkv, gain_pair, shifts[:2])
        width = projected.shape[1] // 3
        memory = jnp.concatenate([projected[:, width:], stale], axis=0)
        attended = attend_tiles(projected, memory, picked, tile_limit.astype(jnp.int32))
        attended = attended.reshape(pair_size, final_rows, width)[order].reshape(rows, width)
        partial = jnp.dot(attended, w_out, preferred_element_type=jnp.float32).astype(
            jnp.bfloat16
        )
        first, second = reduce_two_ways(partial)
        kept = jnp.where(parity == 0, first, second)
        given = jnp.where(parity == 0, second, first)
        received = from_partner(given.astype(jnp.bfloat16), "section", group_bits).astype(
            jnp.float32
        )
        sum_control = jnp.where(parity == 0, kept, received)
        sum_main = jnp.where(parity == 0, received, kept)
        own_start = position * final_rows
        if stage == 0:
            latent_rows = lax.dynamic_slice_in_dim(whole, own_start, final_rows, 0)
            own_embedded = jnp.dot(
                latent_rows[:, :c_out], embed_weight, preferred_element_type=jnp.float32
            )
            control_rows = (
                own_embedded
                + jnp.dot(latent_rows[:, c_out:], control_embed, preferred_element_type=jnp.float32)
            ).astype(jnp.bfloat16)
            hidden_rows = own_embedded.astype(jnp.bfloat16)
        else:
            control_rows = lax.dynamic_slice_in_dim(control_in, own_start, final_rows, 0)
            hidden_rows = lax.dynamic_slice_in_dim(hidden_in, own_start, final_rows, 0)
        control_new = (control_rows.astype(jnp.float32) + gate_control * sum_control).astype(
            jnp.bfloat16
        )
        hidden_new = (
            hidden_rows.astype(jnp.float32)
            + gate_main * sum_main
            + control_row * control_new.astype(jnp.float32)
        ).astype(jnp.bfloat16)
        if stage + 1 < pair_count:
            moved = from_behind((control_new, hidden_new), "section", pair_size)
            control_in = gather_rows(moved[0], position, pair_bits)
            hidden_in = gather_rows(moved[1], position, pair_bits)
            stream = jnp.where(parity == 0, control_in, hidden_in)

    denoised = jnp.dot(
        modulated(hidden_new, final_mod[0], final_mod[1]),
        final_weight,
        preferred_element_type=jnp.float32,
    )
    if pair_count == 1:
        return denoised
    is_last = pair_index == pair_count - 1
    placed = lax.dynamic_update_slice_in_dim(
        jnp.zeros((rows, denoised.shape[1]), jnp.float32),
        jnp.where(is_last, denoised, 0.0),
        position * final_rows,
        0,
    )
    return lax.psum_scatter(placed, "section", scatter_dimension=0, tiled=True)


def solution(mesh):
    return jax.shard_map(
        on_device,
        mesh=mesh,
        in_specs=(
            P(("grp", "section"), None),
            P(("grp", "section"), None),
            P(),
            P(),
            P(),
            P(),
            P(),
            P(),
            P(),
            P("section", None, None),
            P("section", None, None),
            P("section", "grp", None),
            P(),
            P(),
            P(),
        ),
        out_specs=P(("grp", "section"), None),
        check_vma=False,
    )
```

```python
import math

import jax
import jax.numpy as jnp
from jax import lax
from jax.experimental import pallas as pl
from jax.experimental.pallas import tpu as pltpu
from jax.sharding import PartitionSpec as P

HD = 128
HG = 8
TILE = 128

EPSILON = 1e-06


def from_partner(value, axis, distance):
    return lax.ppermute(value, axis, [(i, i ^ 1 << distance) for i in range(lax.axis_size(axis))])


def from_behind(value, axis, steps):
    count = lax.axis_size(axis)
    leading, last = (max(0, -steps), min(count, count - steps))
    return lax.ppermute(value, axis, [(source, source + steps) for source in range(leading, last)])


def modulated(hidden, shift_row, scale_row):
    values = hidden.astype(jnp.float32)
    centered = values - jnp.mean(values, axis=-1, keepdims=True)
    variance = jnp.mean(centered * centered, axis=-1, keepdims=True)
    normed = centered * lax.rsqrt(variance + EPSILON)
    return (normed * (1.0 + scale_row) + shift_row).astype(jnp.bfloat16)


def rms_scaled(values, gain_row):
    return (
        values * lax.rsqrt(jnp.mean(values * values, axis=-1, keepdims=True) + EPSILON) * gain_row
    )


def bit_of(value, bit):
    return (value >> bit) & 1


def gather_rows(mine, position, bit_count):
    gathered = mine
    for bit in range(bit_count):
        partner = from_partner(gathered, "section", bit)
        upper = bit_of(position, bit) == 1
        gathered = jnp.where(
            upper,
            jnp.concatenate([partner, gathered]),
            jnp.concatenate([gathered, partner]),
        )
    return gathered


def qkv_kernel(x_ref, w_ref, g_ref, o_ref):
    j = pl.program_id(0)
    acc = jnp.dot(x_ref[...], w_ref[...], preferred_element_type=jnp.float32)
    gain = g_ref[pl.ds(jnp.minimum(j, 1), 1), :]
    heads = acc.shape[1] // HD
    pieces = []
    for h in range(heads):
        values = acc[:, h * HD : (h + 1) * HD]
        scaled = values * lax.rsqrt(jnp.mean(values * values, axis=-1, keepdims=True) + EPSILON) * gain
        pieces.append(jnp.where(j < 2, scaled, values))
    o_ref[...] = jnp.concatenate(pieces, axis=1).astype(o_ref.dtype)


def project_qkv(modded, w_qkv, gain_pair):
    rows, depth = modded.shape
    width = w_qkv.shape[1] // 3
    return pl.pallas_call(
        qkv_kernel,
        out_shape=jax.ShapeDtypeStruct((rows, 3 * width), jnp.bfloat16),
        grid=(3,),
        in_specs=[
            pl.BlockSpec((rows, depth), lambda j: (0, 0)),
            pl.BlockSpec((depth, width), lambda j: (0, j)),
            pl.BlockSpec((2, HD), lambda j: (0, 0)),
        ],
        out_specs=pl.BlockSpec((rows, width), lambda j: (0, j)),
        compiler_params=pltpu.CompilerParams(vmem_limit_bytes=48 * 1024 * 1024),
        cost_estimate=pl.CostEstimate(
            flops=2 * rows * depth * 3 * width,
            bytes_accessed=2 * (rows * depth + depth * 3 * width + rows * 3 * width),
            transcendentals=0,
        ),
    )(modded, w_qkv, gain_pair)


def attention_kernel(offset_ref, picked_ref, limit_ref, q_ref, m0_ref, m1_ref, m2_ref, o_ref):
    t = pl.program_id(0) + offset_ref[0]
    limit = limit_ref[t]
    width = q_ref.shape[1]
    heads = width // HD
    memories = (m0_ref, m1_ref, m2_ref)
    tile_rows = m0_ref.shape[0]
    key_tile = lax.broadcasted_iota(jnp.int32, (1, len(memories) * tile_rows), 1) // tile_rows
    allowed = key_tile < limit
    for h in range(heads):
        query = q_ref[:, h * HD : (h + 1) * HD]
        keys = jnp.concatenate([m[:, h * HD : (h + 1) * HD] for m in memories], axis=0)
        values = jnp.concatenate(
            [m[:, width + h * HD : width + (h + 1) * HD] for m in memories], axis=0
        )
        scores = lax.dot_general(
            query, keys, (((1,), (1,)), ((), ())), preferred_element_type=jnp.float32
        ) / math.sqrt(HD)
        scores = jnp.where(allowed, scores, -1e30)
        highest = jnp.max(scores, axis=-1, keepdims=True)
        weights = jnp.exp(scores - highest)
        probabilities = (weights / jnp.sum(weights, axis=-1, keepdims=True)).astype(jnp.bfloat16)
        acc = jnp.dot(probabilities, values, preferred_element_type=jnp.float32)
        o_ref[:, h * HD : (h + 1) * HD] = acc.astype(o_ref.dtype)

def gather_all(mine, index, count):
    spread = jnp.broadcast_to(mine[None], (count,) + mine.shape)
    gathered = lax.all_to_all(spread, "section", 0, 0, tiled=False)
    return gathered.reshape((count * mine.shape[0],) + mine.shape[1:])

def attend_tiles(projected, memory, picked, limit, offset, count):
    rows = projected.shape[0]
    width = projected.shape[1] // 3
    mem_width = memory.shape[1]

    def memory_spec(j):
        return pl.BlockSpec((TILE, mem_width), lambda t, o, p, c: (p[t + o[0], j], 0))

    return pl.pallas_call(
        attention_kernel,
        out_shape=jax.ShapeDtypeStruct((count * TILE, width), jnp.bfloat16),
        grid_spec=pltpu.PrefetchScalarGridSpec(
            num_scalar_prefetch=3,
            grid=(count,),
            in_specs=[
                pl.BlockSpec((TILE, width), lambda t, o, p, c: (t + o[0], 0)),
                memory_spec(0),
                memory_spec(1),
                memory_spec(2),
            ],
            out_specs=pl.BlockSpec((TILE, width), lambda t, o, p, c: (t, 0)),
        ),
        cost_estimate=pl.CostEstimate(
            flops=4 * count * TILE * 3 * TILE * width,
            bytes_accessed=2 * (2 * count * TILE * width + 3 * count * TILE * mem_width),
            transcendentals=count * TILE * 3 * TILE * (width // HD),
        ),
    )(offset, picked, limit, projected, memory, memory, memory)

def row_table(group_count):
    table = []
    for g in range(group_count):
        first = [2 * k for k in (g, g ^ 4, g ^ 2, g ^ 6)]
        second = [2 * k + 1 for k in (g, g ^ 2, g ^ 4, g ^ 6)]
        other = [2 * k for k in (g ^ 1, g ^ 5, g ^ 3, g ^ 7)]
        other_second = [2 * k + 1 for k in (g ^ 1, g ^ 3, g ^ 5, g ^ 7)]
        table.append(first + second + other + other_second)
    return table

def reduce_two_ways(partial):
    half = partial.shape[0] // 2
    summed = partial[:half].astype(jnp.float32) + from_partner(
        partial[half:], "section", 0
    ).astype(jnp.float32)
    quarter = half // 2
    first, second = summed[:quarter], summed[quarter:]
    eighth = quarter // 2
    first_sent = first[eighth:].astype(jnp.bfloat16)
    second_sent = second[eighth:].astype(jnp.bfloat16)
    first = first[:eighth] + from_partner(first_sent, "section", 1).astype(jnp.float32)
    second = second[:eighth] + from_partner(second_sent, "section", 2).astype(jnp.float32)
    sixteenth = eighth // 2
    first = first[:sixteenth] + from_partner(
        first[sixteenth:].astype(jnp.bfloat16), "section", 2
    ).astype(jnp.float32)
    second = second[:sixteenth] + from_partner(
        second[sixteenth:].astype(jnp.bfloat16), "section", 1
    ).astype(jnp.float32)
    return first, second


def on_device(
    latent,
    control_latent,
    patch_tiles,
    tile_lists,
    tile_counts,
    embed_weight,
    control_embed,
    modulation,
    qk_gain,
    qkv_weight,
    out_weight,
    stale_cache,
    control_gain,
    final_mod,
    final_weight,
):
    section_size = lax.axis_size("section")
    slot_count = section_size // HG
    pair_count = slot_count // 2
    pair_size = 2 * HG
    device_index = lax.axis_index("section")
    slot_index = device_index // HG
    group_index = device_index % HG
    parity = slot_index % 2
    pair_index = slot_index // 2
    position = device_index % pair_size
    group_bits = HG.bit_length() - 1
    pair_bits = pair_size.bit_length() - 1
    section_bits = section_size.bit_length() - 1

    both = jnp.concatenate([latent, control_latent], axis=1)
    whole = gather_all(both, device_index, section_size)
    rows = whole.shape[0]
    c_out = latent.shape[1]
    tiles = rows // TILE
    final_rows = rows // pair_size
    whole_latent = whole[:, :c_out]
    whole_condition = jnp.where(parity == 0, whole[:, c_out:], jnp.zeros_like(whole[:, c_out:]))
    embedded = jnp.dot(whole_latent, embed_weight, preferred_element_type=jnp.float32)
    stream = (
        embedded + jnp.dot(whole_condition, control_embed, preferred_element_type=jnp.float32)
    ).astype(jnp.bfloat16)
    hidden_in = embedded.astype(jnp.bfloat16)

    starts = jnp.cumsum(patch_tiles) - patch_tiles
    tile_ids = jnp.arange(tiles, dtype=jnp.int32)
    tile_patch = jnp.sum((starts[None, :] <= tile_ids[:, None]).astype(jnp.int32), axis=1) - 1

    w_qkv = qkv_weight[0]
    w_out = out_weight[0]
    stale = stale_cache[0]
    shifts = modulation[slot_index]
    gain_pair = qk_gain[slot_index]
    tile_list = tile_lists[slot_index]
    tile_limit = tile_counts[slot_index]
    use_new = tile_patch[tile_list] <= tile_patch[:, None]
    picked = (tile_list + jnp.where(use_new, 0, tiles)).astype(jnp.int32)
    gate_control = modulation[2 * pair_index, 2]
    gate_main = modulation[2 * pair_index + 1, 2]
    control_row = control_gain[pair_index]
    order = jnp.array(row_table(HG), jnp.int32)[group_index]
    halves = pair_size // HG

    for stage in range(pair_count):
        modded = modulated(stream, shifts[0], shifts[1])
        projected = project_qkv(modded, w_qkv, gain_pair)
        width = projected.shape[1] // 3
        memory = jnp.concatenate([projected[:, width:], stale], axis=0)
        chunk_tiles = tiles // halves
        chunk_rows = rows // halves
        results = []
        for chunk in (1 - parity, parity):
            offset = jnp.reshape(chunk * chunk_tiles, (1,)).astype(jnp.int32)
            attended = attend_tiles(
                projected, memory, picked, tile_limit.astype(jnp.int32), offset, chunk_tiles
            )
            attended = attended.reshape(2 * HG, final_rows // 2, width)[order].reshape(
                chunk_rows, width
            )
            partial = jnp.dot(attended, w_out, preferred_element_type=jnp.float32).astype(
                jnp.bfloat16
            )
            first, second = reduce_two_ways(partial)
            results.append(jnp.concatenate([first, second], axis=0))
        received = from_partner(results[0].astype(jnp.bfloat16), "section", group_bits).astype(
            jnp.float32
        )
        kept = results[1]
        sum_control = jnp.where(parity == 0, kept, received)
        sum_main = jnp.where(parity == 0, received, kept)
        own_start = position * final_rows
        if stage == 0:
            latent_rows = lax.dynamic_slice_in_dim(whole, own_start, final_rows, 0)
            own_embedded = jnp.dot(
                latent_rows[:, :c_out], embed_weight, preferred_element_type=jnp.float32
            )
            control_rows = (
                own_embedded
                + jnp.dot(latent_rows[:, c_out:], control_embed, preferred_element_type=jnp.float32)
            ).astype(jnp.bfloat16)
            hidden_rows = own_embedded.astype(jnp.bfloat16)
        else:
            control_rows = lax.dynamic_slice_in_dim(control_in, own_start, final_rows, 0)
            hidden_rows = lax.dynamic_slice_in_dim(hidden_in, own_start, final_rows, 0)
        control_new = (control_rows.astype(jnp.float32) + gate_control * sum_control).astype(
            jnp.bfloat16
        )
        hidden_new = (
            hidden_rows.astype(jnp.float32)
            + gate_main * sum_main
            + control_row * control_new.astype(jnp.float32)
        ).astype(jnp.bfloat16)
        if stage + 1 < pair_count:
            moved = from_behind((control_new, hidden_new), "section", pair_size)
            control_in = gather_rows(moved[0], position, pair_bits)
            hidden_in = gather_rows(moved[1], position, pair_bits)
            stream = jnp.where(parity == 0, control_in, hidden_in)

    denoised = jnp.dot(
        modulated(hidden_new, final_mod[0], final_mod[1]),
        final_weight,
        preferred_element_type=jnp.float32,
    )
    if pair_count == 1:
        return denoised
    is_last = pair_index == pair_count - 1
    placed = lax.dynamic_update_slice_in_dim(
        jnp.zeros((rows, denoised.shape[1]), jnp.float32),
        jnp.where(is_last, denoised, 0.0),
        position * final_rows,
        0,
    )
    return lax.psum_scatter(placed, "section", scatter_dimension=0, tiled=True)


def solution(mesh):
    return jax.shard_map(
        on_device,
        mesh=mesh,
        in_specs=(
            P(("grp", "section"), None),
            P(("grp", "section"), None),
            P(),
            P(),
            P(),
            P(),
            P(),
            P(),
            P(),
            P("section", None, None),
            P("section", None, None),
            P("section", "grp", None),
            P(),
            P(),
            P(),
        ),
        out_specs=P(("grp", "section"), None),
        check_vma=False,
    )
```

```python
import math

import jax
import jax.numpy as jnp
from jax import lax
from jax.experimental import pallas as pl
from jax.experimental.pallas import tpu as pltpu
from jax.sharding import PartitionSpec as P

HD = 128
HG = 8
TILE = 128

EPSILON = 1e-06


def from_partner(value, axis, distance):
    return lax.ppermute(value, axis, [(i, i ^ 1 << distance) for i in range(lax.axis_size(axis))])


def from_behind(value, axis, steps):
    count = lax.axis_size(axis)
    leading, last = (max(0, -steps), min(count, count - steps))
    return lax.ppermute(value, axis, [(source, source + steps) for source in range(leading, last)])


def modulated(hidden, shift_row, scale_row):
    values = hidden.astype(jnp.float32)
    centered = values - jnp.mean(values, axis=-1, keepdims=True)
    variance = jnp.mean(centered * centered, axis=-1, keepdims=True)
    normed = centered * lax.rsqrt(variance + EPSILON)
    return (normed * (1.0 + scale_row) + shift_row).astype(jnp.bfloat16)


def rms_scaled(values, gain_row):
    return (
        values * lax.rsqrt(jnp.mean(values * values, axis=-1, keepdims=True) + EPSILON) * gain_row
    )


def bit_of(value, bit):
    return (value >> bit) & 1


def gather_rows(mine, position, bit_count):
    gathered = mine
    for bit in range(bit_count):
        partner = from_partner(gathered, "section", bit)
        upper = bit_of(position, bit) == 1
        gathered = jnp.where(
            upper,
            jnp.concatenate([partner, gathered]),
            jnp.concatenate([gathered, partner]),
        )
    return gathered


def qkv_kernel(x_ref, w_ref, g_ref, o_ref):
    j = pl.program_id(0)
    acc = jnp.dot(x_ref[...], w_ref[...], preferred_element_type=jnp.float32)
    gain = g_ref[pl.ds(jnp.minimum(j, 1), 1), :]
    heads = acc.shape[1] // HD
    pieces = []
    for h in range(heads):
        values = acc[:, h * HD : (h + 1) * HD]
        scaled = values * lax.rsqrt(jnp.mean(values * values, axis=-1, keepdims=True) + EPSILON) * gain
        pieces.append(jnp.where(j < 2, scaled, values))
    o_ref[...] = jnp.concatenate(pieces, axis=1).astype(o_ref.dtype)


def project_qkv(modded, w_qkv, gain_pair):
    rows, depth = modded.shape
    width = w_qkv.shape[1] // 3
    return pl.pallas_call(
        qkv_kernel,
        out_shape=jax.ShapeDtypeStruct((rows, 3 * width), jnp.bfloat16),
        grid=(3,),
        in_specs=[
            pl.BlockSpec((rows, depth), lambda j: (0, 0)),
            pl.BlockSpec((depth, width), lambda j: (0, j)),
            pl.BlockSpec((2, HD), lambda j: (0, 0)),
        ],
        out_specs=pl.BlockSpec((rows, width), lambda j: (0, j)),
        compiler_params=pltpu.CompilerParams(vmem_limit_bytes=48 * 1024 * 1024),
        cost_estimate=pl.CostEstimate(
            flops=2 * rows * depth * 3 * width,
            bytes_accessed=2 * (rows * depth + depth * 3 * width + rows * 3 * width),
            transcendentals=0,
        ),
    )(modded, w_qkv, gain_pair)


def qkv_embed_kernel(lat_ref, cond_ref, e_ref, c_ref, w_ref, g_ref, m_ref, o_ref, n_ref):
    j = pl.program_id(0)
    chunk = 64

    @pl.when(j == 0)
    def _():
        shift = m_ref[0:1, :]
        scale = 1.0 + m_ref[1:2, :]

        def body(i, carry):
            r = pl.ds(pl.multiple_of(i * chunk, chunk), chunk)
            embedded = jnp.dot(lat_ref[r, :], e_ref[...], preferred_element_type=jnp.float32)
            embedded = embedded + jnp.dot(
                cond_ref[r, :], c_ref[...], preferred_element_type=jnp.float32
            )
            values = embedded.astype(jnp.bfloat16).astype(jnp.float32)
            centered = values - jnp.mean(values, axis=-1, keepdims=True)
            variance = jnp.mean(centered * centered, axis=-1, keepdims=True)
            normed = centered * lax.rsqrt(variance + EPSILON)
            n_ref[r, :] = (normed * scale + shift).astype(n_ref.dtype)
            return carry

        lax.fori_loop(0, lat_ref.shape[0] // chunk, body, 0)

    acc = jnp.dot(n_ref[...], w_ref[...], preferred_element_type=jnp.float32)
    gain = g_ref[pl.ds(jnp.minimum(j, 1), 1), :]
    heads = acc.shape[1] // HD
    pieces = []
    for h in range(heads):
        values = acc[:, h * HD : (h + 1) * HD]
        scaled = values * lax.rsqrt(jnp.mean(values * values, axis=-1, keepdims=True) + EPSILON) * gain
        pieces.append(jnp.where(j < 2, scaled, values))
    o_ref[...] = jnp.concatenate(pieces, axis=1).astype(o_ref.dtype)


def project_embedded(latents, condition, embed, control_embed, w_qkv, gain_pair, shift_scale):
    rows, c_in = latents.shape
    depth = embed.shape[1]
    width = w_qkv.shape[1] // 3
    return pl.pallas_call(
        qkv_embed_kernel,
        out_shape=jax.ShapeDtypeStruct((rows, 3 * width), jnp.bfloat16),
        grid=(3,),
        in_specs=[
            pl.BlockSpec((rows, c_in), lambda j: (0, 0)),
            pl.BlockSpec((rows, c_in), lambda j: (0, 0)),
            pl.BlockSpec((c_in, depth), lambda j: (0, 0)),
            pl.BlockSpec((c_in, depth), lambda j: (0, 0)),
            pl.BlockSpec((depth, width), lambda j: (0, j)),
            pl.BlockSpec((2, HD), lambda j: (0, 0)),
            pl.BlockSpec((2, depth), lambda j: (0, 0)),
        ],
        out_specs=pl.BlockSpec((rows, width), lambda j: (0, j)),
        scratch_shapes=[pltpu.VMEM((rows, depth), jnp.bfloat16)],
        compiler_params=pltpu.CompilerParams(
            dimension_semantics=("arbitrary",), vmem_limit_bytes=48 * 1024 * 1024
        ),
        cost_estimate=pl.CostEstimate(
            flops=2 * rows * depth * (3 * width + 2 * c_in),
            bytes_accessed=2 * (2 * rows * c_in + depth * 3 * width + rows * 3 * width),
            transcendentals=0,
        ),
    )(latents, condition, embed, control_embed, w_qkv, gain_pair, shift_scale)


def attention_kernel(picked_ref, limit_ref, q_ref, m0_ref, m1_ref, m2_ref, o_ref):
    t = pl.program_id(0)
    limit = limit_ref[t]
    width = q_ref.shape[1]
    heads = width // HD
    memories = (m0_ref, m1_ref, m2_ref)
    tile_rows = m0_ref.shape[0]
    key_tile = lax.broadcasted_iota(jnp.int32, (1, len(memories) * tile_rows), 1) // tile_rows
    allowed = key_tile < limit
    for h in range(heads):
        query = q_ref[:, h * HD : (h + 1) * HD]
        keys = jnp.concatenate([m[:, h * HD : (h + 1) * HD] for m in memories], axis=0)
        values = jnp.concatenate(
            [m[:, width + h * HD : width + (h + 1) * HD] for m in memories], axis=0
        )
        scores = lax.dot_general(
            query, keys, (((1,), (1,)), ((), ())), preferred_element_type=jnp.float32
        ) / math.sqrt(HD)
        scores = jnp.where(allowed, scores, -1e30)
        highest = jnp.max(scores, axis=-1, keepdims=True)
        weights = jnp.exp(scores - highest)
        probabilities = (weights / jnp.sum(weights, axis=-1, keepdims=True)).astype(jnp.bfloat16)
        acc = jnp.dot(probabilities, values, preferred_element_type=jnp.float32)
        o_ref[:, h * HD : (h + 1) * HD] = acc.astype(o_ref.dtype)

def gather_all(mine, index, count):
    spread = jnp.broadcast_to(mine[None], (count,) + mine.shape)
    gathered = lax.all_to_all(spread, "section", 0, 0, tiled=False)
    return gathered.reshape((count * mine.shape[0],) + mine.shape[1:])

def attend_tiles(projected, memory, picked, limit):
    rows = projected.shape[0]
    width = projected.shape[1] // 3
    tiles = rows // TILE
    mem_width = memory.shape[1]

    def memory_spec(j):
        return pl.BlockSpec((TILE, mem_width), lambda t, p, c: (p[t, j], 0))

    return pl.pallas_call(
        attention_kernel,
        out_shape=jax.ShapeDtypeStruct((rows, width), jnp.bfloat16),
        grid_spec=pltpu.PrefetchScalarGridSpec(
            num_scalar_prefetch=2,
            grid=(tiles,),
            in_specs=[
                pl.BlockSpec((TILE, width), lambda t, p, c: (t, 0)),
                memory_spec(0),
                memory_spec(1),
                memory_spec(2),
            ],
            out_specs=pl.BlockSpec((TILE, width), lambda t, p, c: (t, 0)),
        ),
        cost_estimate=pl.CostEstimate(
            flops=4 * rows * 3 * TILE * width,
            bytes_accessed=2 * (2 * rows * width + 3 * rows * mem_width),
            transcendentals=rows * 3 * TILE * (width // HD),
        ),
    )(picked, limit, projected, memory, memory, memory)


def row_table(group_count):
    table = []
    for g in range(group_count):
        first = [g, g ^ 4, g ^ 2, g ^ 6]
        second = [group_count + k for k in (g, g ^ 2, g ^ 4, g ^ 6)]
        own = first + second
        other = [g ^ 1, g ^ 5, g ^ 3, g ^ 7]
        other_second = [group_count + k for k in (g ^ 1, g ^ 3, g ^ 5, g ^ 7)]
        table.append(own + other + other_second)
    return table


def reduce_two_ways(partial):
    half = partial.shape[0] // 2
    summed = partial[:half].astype(jnp.float32) + from_partner(
        partial[half:], "section", 0
    ).astype(jnp.float32)
    quarter = half // 2
    first, second = summed[:quarter], summed[quarter:]
    eighth = quarter // 2
    first_sent = first[eighth:].astype(jnp.bfloat16)
    second_sent = second[eighth:].astype(jnp.bfloat16)
    first = first[:eighth] + from_partner(first_sent, "section", 1).astype(jnp.float32)
    second = second[:eighth] + from_partner(second_sent, "section", 2).astype(jnp.float32)
    sixteenth = eighth // 2
    first = first[:sixteenth] + from_partner(
        first[sixteenth:].astype(jnp.bfloat16), "section", 2
    ).astype(jnp.float32)
    second = second[:sixteenth] + from_partner(
        second[sixteenth:].astype(jnp.bfloat16), "section", 1
    ).astype(jnp.float32)
    return first, second


def on_device(
    latent,
    control_latent,
    patch_tiles,
    tile_lists,
    tile_counts,
    embed_weight,
    control_embed,
    modulation,
    qk_gain,
    qkv_weight,
    out_weight,
    stale_cache,
    control_gain,
    final_mod,
    final_weight,
):
    section_size = lax.axis_size("section")
    slot_count = section_size // HG
    pair_count = slot_count // 2
    pair_size = 2 * HG
    device_index = lax.axis_index("section")
    slot_index = device_index // HG
    group_index = device_index % HG
    parity = slot_index % 2
    pair_index = slot_index // 2
    position = device_index % pair_size
    group_bits = HG.bit_length() - 1
    pair_bits = pair_size.bit_length() - 1
    section_bits = section_size.bit_length() - 1

    both = jnp.concatenate([latent, control_latent], axis=1)
    whole = gather_all(both, device_index, section_size)
    rows = whole.shape[0]
    c_out = latent.shape[1]
    tiles = rows // TILE
    final_rows = rows // pair_size
    whole_latent = whole[:, :c_out]
    whole_condition = jnp.where(parity == 0, whole[:, c_out:], jnp.zeros_like(whole[:, c_out:]))
    stream = None

    starts = jnp.cumsum(patch_tiles) - patch_tiles
    tile_ids = jnp.arange(tiles, dtype=jnp.int32)
    tile_patch = jnp.sum((starts[None, :] <= tile_ids[:, None]).astype(jnp.int32), axis=1) - 1

    w_qkv = qkv_weight[0]
    w_out = out_weight[0]
    stale = stale_cache[0]
    shifts = modulation[slot_index]
    gain_pair = qk_gain[slot_index]
    tile_list = tile_lists[slot_index]
    tile_limit = tile_counts[slot_index]
    use_new = tile_patch[tile_list] <= tile_patch[:, None]
    picked = (tile_list + jnp.where(use_new, 0, tiles)).astype(jnp.int32)
    gate_control = modulation[2 * pair_index, 2]
    gate_main = modulation[2 * pair_index + 1, 2]
    control_row = control_gain[pair_index]
    order = jnp.array(row_table(HG), jnp.int32)[group_index]

    for stage in range(pair_count):
        if stage == 0:
            projected = project_embedded(
                whole_latent, whole_condition, embed_weight, control_embed, w_qkv, gain_pair,
                shifts[:2],
            )
        else:
            modded = modulated(stream, shifts[0], shifts[1])
            projected = project_qkv(modded, w_qkv, gain_pair)
        width = projected.shape[1] // 3
        memory = jnp.concatenate([projected[:, width:], stale], axis=0)
        attended = attend_tiles(projected, memory, picked, tile_limit.astype(jnp.int32))
        attended = attended.reshape(pair_size, final_rows, width)[order].reshape(rows, width)
        partial = jnp.dot(attended, w_out, preferred_element_type=jnp.float32).astype(
            jnp.bfloat16
        )
        first, second = reduce_two_ways(partial)
        kept = jnp.where(parity == 0, first, second)
        given = jnp.where(parity == 0, second, first)
        received = from_partner(given.astype(jnp.bfloat16), "section", group_bits).astype(
            jnp.float32
        )
        sum_control = jnp.where(parity == 0, kept, received)
        sum_main = jnp.where(parity == 0, received, kept)
        own_start = position * final_rows
        if stage == 0:
            latent_rows = lax.dynamic_slice_in_dim(whole, own_start, final_rows, 0)
            own_embedded = jnp.dot(
                latent_rows[:, :c_out], embed_weight, preferred_element_type=jnp.float32
            )
            control_rows = (
                own_embedded
                + jnp.dot(latent_rows[:, c_out:], control_embed, preferred_element_type=jnp.float32)
            ).astype(jnp.bfloat16)
            hidden_rows = own_embedded.astype(jnp.bfloat16)
        else:
            control_rows = lax.dynamic_slice_in_dim(control_in, own_start, final_rows, 0)
            hidden_rows = lax.dynamic_slice_in_dim(hidden_in, own_start, final_rows, 0)
        control_new = (control_rows.astype(jnp.float32) + gate_control * sum_control).astype(
            jnp.bfloat16
        )
        hidden_new = (
            hidden_rows.astype(jnp.float32)
            + gate_main * sum_main
            + control_row * control_new.astype(jnp.float32)
        ).astype(jnp.bfloat16)
        if stage + 1 < pair_count:
            moved = from_behind((control_new, hidden_new), "section", pair_size)
            control_in = gather_rows(moved[0], position, pair_bits)
            hidden_in = gather_rows(moved[1], position, pair_bits)
            stream = jnp.where(parity == 0, control_in, hidden_in)

    denoised = jnp.dot(
        modulated(hidden_new, final_mod[0], final_mod[1]),
        final_weight,
        preferred_element_type=jnp.float32,
    )
    if pair_count == 1:
        return denoised
    is_last = pair_index == pair_count - 1
    placed = lax.dynamic_update_slice_in_dim(
        jnp.zeros((rows, denoised.shape[1]), jnp.float32),
        jnp.where(is_last, denoised, 0.0),
        position * final_rows,
        0,
    )
    return lax.psum_scatter(placed, "section", scatter_dimension=0, tiled=True)


def solution(mesh):
    return jax.shard_map(
        on_device,
        mesh=mesh,
        in_specs=(
            P(("grp", "section"), None),
            P(("grp", "section"), None),
            P(),
            P(),
            P(),
            P(),
            P(),
            P(),
            P(),
            P("section", None, None),
            P("section", None, None),
            P("section", "grp", None),
            P(),
            P(),
            P(),
        ),
        out_specs=P(("grp", "section"), None),
        check_vma=False,
    )
```

```python
import math

import jax
import jax.numpy as jnp
from jax import lax
from jax.experimental import pallas as pl
from jax.experimental.pallas import tpu as pltpu
from jax.sharding import PartitionSpec as P

HD = 128
HG = 8
TILE = 128

EPSILON = 1e-06


def from_partner(value, axis, distance):
    return lax.ppermute(value, axis, [(i, i ^ 1 << distance) for i in range(lax.axis_size(axis))])


def from_behind(value, axis, steps):
    count = lax.axis_size(axis)
    leading, last = (max(0, -steps), min(count, count - steps))
    return lax.ppermute(value, axis, [(source, source + steps) for source in range(leading, last)])


def modulated(hidden, shift_row, scale_row):
    values = hidden.astype(jnp.float32)
    centered = values - jnp.mean(values, axis=-1, keepdims=True)
    variance = jnp.mean(centered * centered, axis=-1, keepdims=True)
    normed = centered * lax.rsqrt(variance + EPSILON)
    return (normed * (1.0 + scale_row) + shift_row).astype(jnp.bfloat16)


def rms_scaled(values, gain_row):
    return (
        values * lax.rsqrt(jnp.mean(values * values, axis=-1, keepdims=True) + EPSILON) * gain_row
    )


def bit_of(value, bit):
    return (value >> bit) & 1


def gather_rows(mine, position, bit_count):
    gathered = mine
    for bit in range(bit_count):
        partner = from_partner(gathered, "section", bit)
        upper = bit_of(position, bit) == 1
        gathered = jnp.where(
            upper,
            jnp.concatenate([partner, gathered]),
            jnp.concatenate([gathered, partner]),
        )
    return gathered


def qkv_kernel(x_ref, w_ref, g_ref, o_ref):
    j = pl.program_id(0)
    acc = jnp.dot(x_ref[...], w_ref[...], preferred_element_type=jnp.float32)
    gain = g_ref[pl.ds(jnp.minimum(j, 1), 1), :]
    heads = acc.shape[1] // HD
    pieces = []
    for h in range(heads):
        values = acc[:, h * HD : (h + 1) * HD]
        scaled = values * lax.rsqrt(jnp.mean(values * values, axis=-1, keepdims=True) + EPSILON) * gain
        pieces.append(jnp.where(j < 2, scaled, values))
    o_ref[...] = jnp.concatenate(pieces, axis=1).astype(o_ref.dtype)


def project_qkv(modded, w_qkv, gain_pair):
    rows, depth = modded.shape
    width = w_qkv.shape[1] // 3
    return pl.pallas_call(
        qkv_kernel,
        out_shape=jax.ShapeDtypeStruct((rows, 3 * width), jnp.bfloat16),
        grid=(3,),
        in_specs=[
            pl.BlockSpec((rows, depth), lambda j: (0, 0)),
            pl.BlockSpec((depth, width), lambda j: (0, j)),
            pl.BlockSpec((2, HD), lambda j: (0, 0)),
        ],
        out_specs=pl.BlockSpec((rows, width), lambda j: (0, j)),
        compiler_params=pltpu.CompilerParams(vmem_limit_bytes=48 * 1024 * 1024),
        cost_estimate=pl.CostEstimate(
            flops=2 * rows * depth * 3 * width,
            bytes_accessed=2 * (rows * depth + depth * 3 * width + rows * 3 * width),
            transcendentals=0,
        ),
    )(modded, w_qkv, gain_pair)


def qkv_embed_kernel(lat_ref, cond_ref, e_ref, c_ref, w_ref, g_ref, m_ref, o_ref, n_ref):
    j = pl.program_id(0)
    chunk = 64

    @pl.when(j == 0)
    def _():
        shift = m_ref[0:1, :]
        scale = 1.0 + m_ref[1:2, :]

        def body(i, carry):
            r = pl.ds(pl.multiple_of(i * chunk, chunk), chunk)
            embedded = jnp.dot(lat_ref[r, :], e_ref[...], preferred_element_type=jnp.float32)
            embedded = embedded + jnp.dot(
                cond_ref[r, :], c_ref[...], preferred_element_type=jnp.float32
            )
            values = embedded.astype(jnp.bfloat16).astype(jnp.float32)
            centered = values - jnp.mean(values, axis=-1, keepdims=True)
            variance = jnp.mean(centered * centered, axis=-1, keepdims=True)
            normed = centered * lax.rsqrt(variance + EPSILON)
            n_ref[r, :] = (normed * scale + shift).astype(n_ref.dtype)
            return carry

        lax.fori_loop(0, lat_ref.shape[0] // chunk, body, 0)

    acc = jnp.dot(n_ref[...], w_ref[...], preferred_element_type=jnp.float32)
    gain = g_ref[pl.ds(jnp.minimum(j, 1), 1), :]
    heads = acc.shape[1] // HD
    pieces = []
    for h in range(heads):
        values = acc[:, h * HD : (h + 1) * HD]
        scaled = values * lax.rsqrt(jnp.mean(values * values, axis=-1, keepdims=True) + EPSILON) * gain
        pieces.append(jnp.where(j < 2, scaled, values))
    o_ref[...] = jnp.concatenate(pieces, axis=1).astype(o_ref.dtype)


def project_embedded(latents, condition, embed, control_embed, w_qkv, gain_pair, shift_scale):
    rows, c_in = latents.shape
    depth = embed.shape[1]
    width = w_qkv.shape[1] // 3
    return pl.pallas_call(
        qkv_embed_kernel,
        out_shape=jax.ShapeDtypeStruct((rows, 3 * width), jnp.bfloat16),
        grid=(3,),
        in_specs=[
            pl.BlockSpec((rows, c_in), lambda j: (0, 0)),
            pl.BlockSpec((rows, c_in), lambda j: (0, 0)),
            pl.BlockSpec((c_in, depth), lambda j: (0, 0)),
            pl.BlockSpec((c_in, depth), lambda j: (0, 0)),
            pl.BlockSpec((depth, width), lambda j: (0, j)),
            pl.BlockSpec((2, HD), lambda j: (0, 0)),
            pl.BlockSpec((2, depth), lambda j: (0, 0)),
        ],
        out_specs=pl.BlockSpec((rows, width), lambda j: (0, j)),
        scratch_shapes=[pltpu.VMEM((rows, depth), jnp.bfloat16)],
        compiler_params=pltpu.CompilerParams(
            dimension_semantics=("arbitrary",), vmem_limit_bytes=48 * 1024 * 1024
        ),
        cost_estimate=pl.CostEstimate(
            flops=2 * rows * depth * (3 * width + 2 * c_in),
            bytes_accessed=2 * (2 * rows * c_in + depth * 3 * width + rows * 3 * width),
            transcendentals=0,
        ),
    )(latents, condition, embed, control_embed, w_qkv, gain_pair, shift_scale)


def attention_kernel(picked_ref, limit_ref, q_ref, m0_ref, m1_ref, m2_ref, o_ref):
    t = pl.program_id(0)
    limit = limit_ref[t]
    width = q_ref.shape[1]
    heads = width // HD
    memories = (m0_ref, m1_ref, m2_ref)
    tile_rows = m0_ref.shape[0]
    key_tile = lax.broadcasted_iota(jnp.int32, (1, len(memories) * tile_rows), 1) // tile_rows
    allowed = key_tile < limit
    for h in range(heads):
        query = q_ref[:, h * HD : (h + 1) * HD]
        keys = jnp.concatenate([m[:, h * HD : (h + 1) * HD] for m in memories], axis=0)
        values = jnp.concatenate(
            [m[:, width + h * HD : width + (h + 1) * HD] for m in memories], axis=0
        )
        scores = lax.dot_general(
            query, keys, (((1,), (1,)), ((), ())), preferred_element_type=jnp.float32
        ) / math.sqrt(HD)
        scores = jnp.where(allowed, scores, -1e30)
        highest = jnp.max(scores, axis=-1, keepdims=True)
        weights = jnp.exp(scores - highest)
        probabilities = (weights / jnp.sum(weights, axis=-1, keepdims=True)).astype(jnp.bfloat16)
        acc = jnp.dot(probabilities, values, preferred_element_type=jnp.float32)
        o_ref[:, h * HD : (h + 1) * HD] = acc.astype(o_ref.dtype)

def gather_all(mine, index, count):
    spread = jnp.broadcast_to(mine[None], (count,) + mine.shape)
    gathered = lax.all_to_all(spread, "section", 0, 0, tiled=False)
    return gathered.reshape((count * mine.shape[0],) + mine.shape[1:])

def attend_tiles(projected, memory, picked, limit):
    rows = projected.shape[0]
    width = projected.shape[1] // 3
    tiles = rows // TILE
    mem_width = memory.shape[1]

    def memory_spec(j):
        return pl.BlockSpec((TILE, mem_width), lambda t, p, c: (p[t, j], 0))

    return pl.pallas_call(
        attention_kernel,
        out_shape=jax.ShapeDtypeStruct((rows, width), jnp.bfloat16),
        grid_spec=pltpu.PrefetchScalarGridSpec(
            num_scalar_prefetch=2,
            grid=(tiles,),
            in_specs=[
                pl.BlockSpec((TILE, width), lambda t, p, c: (t, 0)),
                memory_spec(0),
                memory_spec(1),
                memory_spec(2),
            ],
            out_specs=pl.BlockSpec((TILE, width), lambda t, p, c: (t, 0)),
        ),
        cost_estimate=pl.CostEstimate(
            flops=4 * rows * 3 * TILE * width,
            bytes_accessed=2 * (2 * rows * width + 3 * rows * mem_width),
            transcendentals=rows * 3 * TILE * (width // HD),
        ),
    )(picked, limit, projected, memory, memory, memory)


def row_table(group_count):
    table = []
    for g in range(group_count):
        first = [g, g ^ 4, g ^ 2, g ^ 6]
        second = [group_count + k for k in (g, g ^ 2, g ^ 4, g ^ 6)]
        own = first + second
        other = [g ^ 1, g ^ 5, g ^ 3, g ^ 7]
        other_second = [group_count + k for k in (g ^ 1, g ^ 3, g ^ 5, g ^ 7)]
        table.append(own + other + other_second)
    return table


def reduce_two_ways(kept_half, sent_half):
    summed = kept_half.astype(jnp.float32) + from_partner(sent_half, "section", 0).astype(
        jnp.float32
    )
    half = kept_half.shape[0]
    quarter = half // 2
    first, second = summed[:quarter], summed[quarter:]
    eighth = quarter // 2
    first_sent = first[eighth:].astype(jnp.bfloat16)
    second_sent = second[eighth:].astype(jnp.bfloat16)
    first = first[:eighth] + from_partner(first_sent, "section", 1).astype(jnp.float32)
    second = second[:eighth] + from_partner(second_sent, "section", 2).astype(jnp.float32)
    sixteenth = eighth // 2
    first = first[:sixteenth] + from_partner(
        first[sixteenth:].astype(jnp.bfloat16), "section", 2
    ).astype(jnp.float32)
    second = second[:sixteenth] + from_partner(
        second[sixteenth:].astype(jnp.bfloat16), "section", 1
    ).astype(jnp.float32)
    return first, second


def on_device(
    latent,
    control_latent,
    patch_tiles,
    tile_lists,
    tile_counts,
    embed_weight,
    control_embed,
    modulation,
    qk_gain,
    qkv_weight,
    out_weight,
    stale_cache,
    control_gain,
    final_mod,
    final_weight,
):
    section_size = lax.axis_size("section")
    slot_count = section_size // HG
    pair_count = slot_count // 2
    pair_size = 2 * HG
    device_index = lax.axis_index("section")
    slot_index = device_index // HG
    group_index = device_index % HG
    parity = slot_index % 2
    pair_index = slot_index // 2
    position = device_index % pair_size
    group_bits = HG.bit_length() - 1
    pair_bits = pair_size.bit_length() - 1
    section_bits = section_size.bit_length() - 1

    both = jnp.concatenate([latent, control_latent], axis=1)
    whole = gather_all(both, device_index, section_size)
    rows = whole.shape[0]
    c_out = latent.shape[1]
    tiles = rows // TILE
    final_rows = rows // pair_size
    whole_latent = whole[:, :c_out]
    whole_condition = jnp.where(parity == 0, whole[:, c_out:], jnp.zeros_like(whole[:, c_out:]))
    stream = None

    starts = jnp.cumsum(patch_tiles) - patch_tiles
    tile_ids = jnp.arange(tiles, dtype=jnp.int32)
    tile_patch = jnp.sum((starts[None, :] <= tile_ids[:, None]).astype(jnp.int32), axis=1) - 1

    w_qkv = qkv_weight[0]
    w_out = out_weight[0]
    stale = stale_cache[0]
    shifts = modulation[slot_index]
    gain_pair = qk_gain[slot_index]
    tile_list = tile_lists[slot_index]
    tile_limit = tile_counts[slot_index]
    use_new = tile_patch[tile_list] <= tile_patch[:, None]
    picked = (tile_list + jnp.where(use_new, 0, tiles)).astype(jnp.int32)
    gate_control = modulation[2 * pair_index, 2]
    gate_main = modulation[2 * pair_index + 1, 2]
    control_row = control_gain[pair_index]
    order = jnp.array(row_table(HG), jnp.int32)[group_index]

    for stage in range(pair_count):
        if stage == 0:
            projected = project_embedded(
                whole_latent, whole_condition, embed_weight, control_embed, w_qkv, gain_pair,
                shifts[:2],
            )
        else:
            modded = modulated(stream, shifts[0], shifts[1])
            projected = project_qkv(modded, w_qkv, gain_pair)
        width = projected.shape[1] // 3
        memory = jnp.concatenate([projected[:, width:], stale], axis=0)
        attended = attend_tiles(projected, memory, picked, tile_limit.astype(jnp.int32))
        attended = attended.reshape(pair_size, final_rows, width)[order].reshape(rows, width)
        half_rows = rows // 2
        kept_half = jnp.dot(
            attended[:half_rows], w_out, preferred_element_type=jnp.float32
        ).astype(jnp.bfloat16)
        sent_half = jnp.dot(
            attended[half_rows:], w_out, preferred_element_type=jnp.float32
        ).astype(jnp.bfloat16)
        first, second = reduce_two_ways(kept_half, sent_half)
        kept = jnp.where(parity == 0, first, second)
        given = jnp.where(parity == 0, second, first)
        received = from_partner(given.astype(jnp.bfloat16), "section", group_bits).astype(
            jnp.float32
        )
        sum_control = jnp.where(parity == 0, kept, received)
        sum_main = jnp.where(parity == 0, received, kept)
        own_start = position * final_rows
        if stage == 0:
            latent_rows = lax.dynamic_slice_in_dim(whole, own_start, final_rows, 0)
            own_embedded = jnp.dot(
                latent_rows[:, :c_out], embed_weight, preferred_element_type=jnp.float32
            )
            control_rows = (
                own_embedded
                + jnp.dot(latent_rows[:, c_out:], control_embed, preferred_element_type=jnp.float32)
            ).astype(jnp.bfloat16)
            hidden_rows = own_embedded.astype(jnp.bfloat16)
        else:
            control_rows = lax.dynamic_slice_in_dim(control_in, own_start, final_rows, 0)
            hidden_rows = lax.dynamic_slice_in_dim(hidden_in, own_start, final_rows, 0)
        control_new = (control_rows.astype(jnp.float32) + gate_control * sum_control).astype(
            jnp.bfloat16
        )
        hidden_new = (
            hidden_rows.astype(jnp.float32)
            + gate_main * sum_main
            + control_row * control_new.astype(jnp.float32)
        ).astype(jnp.bfloat16)
        if stage + 1 < pair_count:
            moved = from_behind((control_new, hidden_new), "section", pair_size)
            control_in = gather_rows(moved[0], position, pair_bits)
            hidden_in = gather_rows(moved[1], position, pair_bits)
            stream = jnp.where(parity == 0, control_in, hidden_in)

    denoised = jnp.dot(
        modulated(hidden_new, final_mod[0], final_mod[1]),
        final_weight,
        preferred_element_type=jnp.float32,
    )
    if pair_count == 1:
        return denoised
    is_last = pair_index == pair_count - 1
    placed = lax.dynamic_update_slice_in_dim(
        jnp.zeros((rows, denoised.shape[1]), jnp.float32),
        jnp.where(is_last, denoised, 0.0),
        position * final_rows,
        0,
    )
    return lax.psum_scatter(placed, "section", scatter_dimension=0, tiled=True)


def solution(mesh):
    return jax.shard_map(
        on_device,
        mesh=mesh,
        in_specs=(
            P(("grp", "section"), None),
            P(("grp", "section"), None),
            P(),
            P(),
            P(),
            P(),
            P(),
            P(),
            P(),
            P("section", None, None),
            P("section", None, None),
            P("section", "grp", None),
            P(),
            P(),
            P(),
        ),
        out_specs=P(("grp", "section"), None),
        check_vma=False,
    )
```
